256 devices in a mesh: gx: 16 (over x, y), gy: 4 (over z_hi, core), gz: 4 (over z_lo).
Axes of the slice: x: 4, y: 4, z: 8 (z_hi: 2, z_lo: 4; z = z_hi * 4 + z_lo), core: 2. Of those that a mesh axis runs over, the one named last changes fastest.
Arguments:
- populations: float32 [19, 256, 64, 1024], P(None, 'gx', 'gy', 'gz'), may hold values from 0.01 to 0.11
- marker_force: float32 [3, 262144], P(None, ('gx', 'gy', 'gz')), may hold values from -12 to 12
- marker_offset: float32 [3, 262144], P(None, ('gx', 'gy', 'gz')), may hold values from 0 to 1
- marker_owner: int32 [262144, 1], P(('gx', 'gy', 'gz')), may hold values from 0 to 255; in each aligned block of 1024 rows (0 to 1023, 1024 to 2047, ...) at most 8 rows name the same one
- marker_cell: int32 [262144], P(('gx', 'gy', 'gz')), may hold values from 0 to 65535
Outputs:
- new_populations: float32 [19, 256, 64, 1024], P(None, 'gx', 'gy', 'gz')
- marker_velocity: float32 [3, 262144], P(None, ('gx', 'gy', 'gz'))
The draws below stay inside these ranges and needn't reach their ends.
Inputs may be any that keep to these rules, and one draw needn't show every extreme that they name: `marker_owner`: among the 1024 markers of one device no owner is named more than 8 times, and some device names one owner exactly 8 times.
All inputs are finite; a program needn't handle non-finite values.
Results may differ from the reference program's by a relative error of at most 0.00012.
Values sent between devices are 32-bit elements; how exact they have to be, the bound alone decides.
No kernel may reach another device: no remote copies, remote signals or barrier semaphores. Data moves between devices by JAX's collectives and lax.ppermute only.
A program may use at most 128 MiB of HBM per device.

```python
import math
import jax
import jax.numpy as jnp
import numpy as np
from jax import lax

CX = 16
CY = 16
CZ = 256
MARK_DEV = 1024
NX = 256
NY = 64
NZ = 1024
CELLS_DEV = 65536
MARKERS = 262144
CAP = 8
N_GY = 4
N_GZ = 4
DEVICES = 256


def touch_ends(result, own_key, low, high):
    index_at = [jax.random.randint(jax.random.fold_in(own_key, axis), (), 0, length) for axis, length in enumerate(result.shape)]
    longest = result.shape.index(max(result.shape))
    beside = index_at[:longest] + [(index_at[longest] + 1) % result.shape[longest]] + index_at[longest + 1:]
    return result.at[tuple(index_at)].set(low).at[tuple(beside)].set(high)


def shard_levels(rng, shape, pieces, smallest, top_value):
    loudness, own = 1.0, jax.random.fold_in(rng, 6)
    for axis_at, blocks in pieces:
        draws = jnp.exp(jax.random.uniform(jax.random.fold_in(own, axis_at), (blocks,), jnp.float32, smallest / len(pieces), top_value / len(pieces)))
        loudness = loudness * jnp.repeat(draws, shape[axis_at] // blocks).reshape([-1 if axis == axis_at else 1 for axis in range(len(shape))])
    return loudness


def routed_block(rng, own, number, rows, amount, top, bound, slope):
    ranking = jax.random.permutation(rng, amount)
    heavy_load, ordinary = portions_of(amount, rows * top, bound, slope, True), portions_of(amount, rows * top, bound, slope, False)
    places = jnp.arange(amount)

    def named(sizes, turn):
        used = int((sizes > 0).sum())
        fixed = max(1, used // 4)
        moved = fixed + (places - fixed + turn * (used - fixed)) % max(1, amount - fixed)
        return jnp.zeros((amount,), jnp.int32).at[ranking[jnp.where(places < fixed, places, moved)]].set(jnp.asarray(sizes, jnp.int32))

    sizes = jnp.where(number % 4 == 0, named(heavy_load, number // 4), named(ordinary, number - number // 4 - 1))
    mixed = jax.random.permutation(jax.random.fold_in(own, 3), amount)
    donor, receiver = mixed[0:amount // 2 * 2:2], mixed[1:amount // 2 * 2:2]
    room = jnp.minimum(sizes[donor] - 1, bound - sizes[receiver]) // 2
    room = jnp.where((donor == ranking[0]) | (receiver == ranking[0]) | (sizes[receiver] == 0), 0, jnp.maximum(room, 0))
    moved = jax.random.randint(jax.random.fold_in(own, 4), (amount // 2,), 0, 1 << 20) % (room + 1)
    sizes = sizes.at[donor].add(-moved).at[receiver].add(moved)
    members = jnp.searchsorted(jnp.cumsum(sizes), jnp.arange(rows * top), side="right").astype(jnp.int32)
    grid = members.reshape(top, rows).T
    grid = grid[jax.random.permutation(jax.random.fold_in(own, 1), rows)]
    turn = jax.random.randint(jax.random.fold_in(own, 2), (rows, 1), 0, top)
    return jnp.take_along_axis(grid, (jnp.arange(top)[None, :] + turn) % top, axis=1)


def portions_of(amount, total, reach, skew, full):
    portions = [(1 << 20) // math.isqrt(standing ** skew) + 1 for standing in range(1, amount + 1)]
    largest = reach if full else min(reach, max(-(-total // amount), total * portions[0] // sum(portions)))
    least = 1 if total - largest >= amount - 1 else 0
    holding, surplus = [largest] + [least] * (amount - 1), total - largest - least * (amount - 1)
    while surplus > 0:
        movable = [i for i in range(1, amount) if holding[i] < largest] or [i for i in range(1, amount) if holding[i] < reach]
        whole, budget = sum([portions[i] for i in movable]), surplus
        for i in movable:
            addition = min(reach - holding[i], max(1, budget * portions[i] // whole), surplus)
            holding[i] = holding[i] + addition
            surplus = surplus - addition
    return np.array(holding)


def gaussian(stream_key, shape, scale, bound, cuts=(), held_as=jnp.bfloat16):
    entries = jax.random.normal(stream_key, shape, jnp.float32) * scale
    if len(cuts) > 0:
        entries = shard_levels(stream_key, shape, cuts, -0.22, 0.18) * entries
    return jnp.clip(entries, min=-bound, max=bound).astype(held_as)


def setup_inputs(seed: int = 0) -> dict:
    splits = jax.random.split(jax.random.key(seed), 6)
    populations = jnp.clip(0.01 + 0.1 * jax.random.uniform(splits[0], (19, NX, NY, NZ), jnp.float32) ** shard_levels(splits[0], (19, NX, NY, NZ), ((1, 16), (2, 4), (3, 4)), -0.2, 0.2), 0.01, 0.11)
    marker_force = gaussian(splits[1], (3, MARKERS), 3.0, 12.0, ((1, 256),), jnp.float32)
    marker_offset = jnp.clip(1.0 * jax.random.uniform(splits[2], (3, MARKERS), jnp.float32) ** shard_levels(splits[2], (3, MARKERS), ((1, 256),), -0.2, 0.2), 0.0, 1.0)
    marker_owner_keys = jax.random.split(jax.random.fold_in(splits[3], 1), MARKERS // MARK_DEV)
    marker_owner_turns = jax.random.permutation(jax.random.fold_in(splits[3], 3), MARKERS // MARK_DEV)
    marker_owner = jax.vmap(lambda own, number: routed_block(jax.random.fold_in(splits[3], 2), own, number, MARK_DEV, DEVICES, 1, CAP, 2))(marker_owner_keys, marker_owner_turns).reshape((MARKERS, 1))
    marker_cell = touch_ends(jax.random.randint(splits[4], (MARKERS,), 0, CELLS_DEV), jax.random.fold_in(splits[4], 1), 0, CELLS_DEV - 1).astype(jnp.int32)
    return dict(populations=populations, marker_force=marker_force, marker_offset=marker_offset, marker_owner=marker_owner, marker_cell=marker_cell)


lattice_speeds = ((0, 0, 0), (1, 0, 0), (-1, 0, 0), (0, 1, 0), (0, -1, 0), (0, 0, 1), (0, 0, -1), (1, 1, 0), (-1, -1, 0), (1, -1, 0), (-1, 1, 0), (1, 0, 1), (-1, 0, -1), (1, 0, -1), (-1, 0, 1), (0, 1, 1), (0, -1, -1), (0, 1, -1), (0, -1, 1))
lattice_weights = (1.0 / 3.0,) + (1.0 / 18.0,) * 6 + (1.0 / 36.0,) * 12
relaxation = 0.8

def kernel_weights(offset):
    root_term = jnp.sqrt(1.0 + 4.0 * offset - 4.0 * offset * offset)
    return jnp.stack([(3.0 - 2.0 * offset - root_term) / 8.0, (3.0 - 2.0 * offset + root_term) / 8.0, (1.0 + 2.0 * offset + root_term) / 8.0, (1.0 + 2.0 * offset - root_term) / 8.0])

def collide(populations, forcing):
    density = lax.optimization_barrier(jnp.sum(populations, axis=0))
    velocity = []
    for component in range(3):
        running = 0.5 * forcing[component]
        for direction in range(19):
            speed_value = lattice_speeds[direction][component]
            if speed_value != 0:
                running = running + speed_value * populations[direction]
        velocity.append(running / density)
    square = velocity[0] * velocity[0] + velocity[1] * velocity[1] + velocity[2] * velocity[2]
    collided = []
    for direction in range(19):
        speeds = lattice_speeds[direction]
        weight = lattice_weights[direction]
        contracted = jnp.zeros_like(density)
        for component in range(3):
            if speeds[component] != 0:
                contracted = contracted + speeds[component] * velocity[component]
        equilibrium = weight * density * (1.0 + 3.0 * contracted + 4.5 * contracted * contracted - 1.5 * square)
        source = jnp.zeros_like(density)
        for component in range(3):
            source = source + (3.0 * (speeds[component] - velocity[component]) + 9.0 * contracted * speeds[component]) * forcing[component]
        present = populations[direction]
        collided.append(present - (present - equilibrium) / relaxation + (1.0 - 0.5 / relaxation) * weight * source)
    return (jnp.stack(collided), jnp.stack(velocity))

def reference(populations, marker_force, marker_offset, marker_owner, marker_cell):
    owners = marker_owner[:, 0]
    per_slab = N_GY * N_GZ
    base_first = owners // per_slab * CX + marker_cell // (CY * CZ)
    base_second = owners // N_GZ % N_GY * CY + marker_cell // CZ % CY
    base_third = owners % N_GZ * CZ + marker_cell % CZ
    shifts = jnp.arange(4, dtype=jnp.int32)
    index_first = (base_first[None, :] - 1 + shifts[:, None]) % NX
    index_second = (base_second[None, :] - 1 + shifts[:, None]) % NY
    index_third = (base_third[None, :] - 1 + shifts[:, None]) % NZ
    flat_index = (index_first[:, None, None, :] * NY + index_second[None, :, None, :]) * NZ + index_third[None, None, :, :]
    flat_index = flat_index.reshape(-1).astype(jnp.int32)
    weight_first = kernel_weights(marker_offset[0])
    weight_second = kernel_weights(marker_offset[1])
    weight_third = kernel_weights(marker_offset[2])
    kernel = weight_first[:, None, None, :] * weight_second[None, :, None, :] * weight_third[None, None, :, :]
    kernel = kernel.reshape(64, -1)
    values = (marker_force[:, None, :] * kernel[None]).reshape(3, -1)
    forcing = jnp.zeros((3, NX * NY * NZ), jnp.float32).at[:, flat_index].add(values)
    forcing = forcing.reshape(3, NX, NY, NZ)
    collided, velocity = collide(populations, forcing)
    passed = []
    for direction in range(19):
        passed.append(jnp.roll(collided[direction], lattice_speeds[direction], axis=(0, 1, 2)))
    new_populations = jnp.stack(passed)
    gathered = velocity.reshape(3, -1)[:, flat_index].reshape(3, 64, -1)
    marker_velocity = lax.optimization_barrier(jnp.sum(gathered * kernel[None], axis=1))
    return (new_populations, marker_velocity)
```

```python
import jax
import jax.numpy as jnp
from jax import lax
from jax.sharding import PartitionSpec as P

CX = 16
CY = 16
CZ = 256
MARK_DEV = 1024


lattice_speeds = (
    (0, 0, 0),
    (1, 0, 0),
    (-1, 0, 0),
    (0, 1, 0),
    (0, -1, 0),
    (0, 0, 1),
    (0, 0, -1),
    (1, 1, 0),
    (-1, -1, 0),
    (1, -1, 0),
    (-1, 1, 0),
    (1, 0, 1),
    (-1, 0, -1),
    (1, 0, -1),
    (-1, 0, 1),
    (0, 1, 1),
    (0, -1, -1),
    (0, 1, -1),
    (0, -1, 1),
)
lattice_weights = (1.0 / 3.0,) + (1.0 / 18.0,) * 6 + (1.0 / 36.0,) * 12
relaxation = 0.8
highest = lax.Precision.HIGHEST


def extended_2(cells, sides, width):
    for axis, dim in sides:
        count = lax.axis_size(axis)
        head = lax.slice_in_dim(cells, 0, width, axis=dim)
        tail = lax.slice_in_dim(cells, cells.shape[dim] - width, cells.shape[dim], axis=dim)
        cells = jnp.concatenate(
            [
                lax.ppermute(tail, axis, [(i, (i + 1) % count) for i in range(count)]),
                cells,
                lax.ppermute(head, axis, [((i + 1) % count, i) for i in range(count)]),
            ],
            axis=dim,
        )
    return cells


def kernel_weights(offset):
    root_term = jnp.sqrt(1.0 + 4.0 * offset - 4.0 * offset * offset)
    return jnp.stack(
        [
            (3.0 - 2.0 * offset - root_term) / 8.0,
            (3.0 - 2.0 * offset + root_term) / 8.0,
            (1.0 + 2.0 * offset + root_term) / 8.0,
            (1.0 + 2.0 * offset - root_term) / 8.0,
        ]
    )


def collide(populations, forcing):
    density = jnp.sum(populations, axis=0)
    velocity = []
    for component in range(3):
        running = 0.5 * forcing[component]
        for direction in range(19):
            speed_value = lattice_speeds[direction][component]
            if speed_value != 0:
                running = running + speed_value * populations[direction]
        velocity.append(running / density)
    square = velocity[0] * velocity[0] + velocity[1] * velocity[1] + velocity[2] * velocity[2]
    collided = []
    for direction in range(19):
        speeds = lattice_speeds[direction]
        weight = lattice_weights[direction]
        contracted = jnp.zeros_like(density)
        for component in range(3):
            if speeds[component] != 0:
                contracted = contracted + speeds[component] * velocity[component]
        equilibrium = (
            weight
            * density
            * (1.0 + 3.0 * contracted + 4.5 * contracted * contracted - 1.5 * square)
        )
        source = jnp.zeros_like(density)
        for component in range(3):
            source = (
                source
                + (
                    3.0 * (speeds[component] - velocity[component])
                    + 9.0 * contracted * speeds[component]
                )
                * forcing[component]
            )
        present = populations[direction]
        collided.append(
            present
            - (present - equilibrium) / relaxation
            + (1.0 - 0.5 / relaxation) * weight * source
        )
    return (jnp.stack(collided), jnp.stack(velocity))


def fold_rims(extended, which, extent):
    middle = lax.slice_in_dim(extended, 3, extent + 3, axis=which)
    low_rims = lax.slice_in_dim(extended, 0, 2, axis=which)
    high_rims = lax.slice_in_dim(extended, extent + 5, extent + 6, axis=which)
    low_pad = [(0, 0)] * extended.ndim
    low_pad[which] = (0, extent - 2)
    high_pad = [(0, 0)] * extended.ndim
    high_pad[which] = (extent - 1, 0)
    return middle + jnp.pad(low_rims, low_pad) + jnp.pad(high_rims, high_pad)


def band_matrix(coordinate, weight, extent, anchor):
    positions = lax.broadcasted_iota(jnp.int32, (coordinate.shape[0], extent), 1)
    running = jnp.zeros((coordinate.shape[0], extent), jnp.float32)
    for shift_step in range(4):
        running = running + jnp.where(
            positions == (coordinate + anchor + shift_step)[:, None],
            weight[shift_step][:, None],
            0.0,
        )
    return running


def spread_banded(forces, coordinates, weights, grid_sizes):
    band_first = band_matrix(coordinates[0], weights[0], grid_sizes[0], 0)
    band_second = band_matrix(coordinates[1], weights[1], grid_sizes[1], 0)
    band_third = band_matrix(coordinates[2], weights[2], grid_sizes[2], 0)
    partial_value = (
        forces[:, None, None, :]
        * band_first.T[None, :, None, :]
        * band_second.T[None, None, :, :]
    )
    partial_value = partial_value.reshape(-1, forces.shape[1])
    product = jnp.dot(
        partial_value, band_third, precision=highest, preferred_element_type=jnp.float32
    )
    return product.reshape((3,) + grid_sizes)


def sample_banded(velocity_ext, coordinates, weights, grid_sizes):
    flat_velocity = velocity_ext.reshape(3 * grid_sizes[0] * grid_sizes[1], grid_sizes[2])
    band_first = band_matrix(coordinates[0], weights[0], grid_sizes[0], 1)
    band_second = band_matrix(coordinates[1], weights[1], grid_sizes[1], 1)
    band_third = band_matrix(coordinates[2], weights[2], grid_sizes[2], 1)
    contracted = jnp.dot(
        flat_velocity, band_third.T, precision=highest, preferred_element_type=jnp.float32
    )
    contracted = contracted.reshape(3, grid_sizes[0], grid_sizes[1], -1)
    return jnp.sum(
        contracted * band_first.T[None, :, None, :] * band_second.T[None, None, :, :],
        axis=(1, 2),
    )


def shards(populations, marker_force, marker_offset, marker_owner, marker_cell):
    count_first = lax.axis_size("gx")
    count_rest = lax.axis_size("gy") * lax.axis_size("gz")
    devices = count_first * count_rest
    capacity = max(4, 2 * MARK_DEV // devices)
    slot_count = devices * capacity
    owners = marker_owner[:, 0]
    row_order = lax.broadcasted_iota(jnp.int32, (MARK_DEV, MARK_DEV), 0)
    column_order = lax.broadcasted_iota(jnp.int32, (MARK_DEV, MARK_DEV), 1)
    earlier = (owners[:, None] == owners[None, :]) & (column_order < row_order)
    before = jnp.sum(earlier.astype(jnp.int32), axis=1)
    slot_index = owners * capacity + before
    placing = (
        slot_index[:, None] == lax.broadcasted_iota(jnp.int32, (MARK_DEV, slot_count), 1)
    ).astype(jnp.float32)
    record = jnp.concatenate(
        [marker_offset, marker_force, marker_cell.astype(jnp.float32)[None, :]], axis=0
    )
    buckets = jnp.dot(record, placing, precision=highest, preferred_element_type=jnp.float32)
    buckets = buckets.reshape(7, count_first, count_rest, capacity)
    received = lax.all_to_all(
        lax.all_to_all(buckets, "gx", split_axis=1, concat_axis=1, tiled=True),
        ("gy", "gz"),
        split_axis=2,
        concat_axis=2,
        tiled=True,
    )
    received = received.reshape(7, slot_count)
    forces = received[3:6]
    cell_index = received[6].astype(jnp.int32)
    coordinates = (cell_index // (CY * CZ), cell_index // CZ % CY, cell_index % CZ)
    weights = (
        kernel_weights(received[0]),
        kernel_weights(received[1]),
        kernel_weights(received[2]),
    )
    ghost_sizes = (CX + 3, CY + 3, CZ + 3)
    halo_sizes = (CX + 4, CY + 4, CZ + 4)
    ghost_field = spread_banded(forces, coordinates, weights, ghost_sizes)
    force_halo = extended_2(ghost_field, (("gx", 1), ("gy", 2), ("gz", 3)), 2)
    forcing = fold_rims(fold_rims(fold_rims(force_halo, 1, CX), 2, CY), 3, CZ)
    collided, velocity = collide(populations, forcing)
    collided_ext = extended_2(collided, (("gx", 1), ("gy", 2), ("gz", 3)), 1)
    velocity_ext = extended_2(velocity, (("gx", 1), ("gy", 2), ("gz", 3)), 2)
    margin = 1
    passed = []
    for direction in range(19):
        speeds = lattice_speeds[direction]
        lower_corner = (margin - speeds[0], margin - speeds[1], margin - speeds[2])
        upper_corner = (lower_corner[0] + CX, lower_corner[1] + CY, lower_corner[2] + CZ)
        passed.append(lax.slice(collided_ext[direction], lower_corner, upper_corner))
    new_populations = jnp.stack(passed)
    sampled = sample_banded(velocity_ext, coordinates, weights, halo_sizes)
    sampled = sampled.reshape(3, count_first, count_rest, capacity)
    returned = lax.all_to_all(
        lax.all_to_all(sampled, "gx", split_axis=1, concat_axis=1, tiled=True),
        ("gy", "gz"),
        split_axis=2,
        concat_axis=2,
        tiled=True,
    )
    returned = returned.reshape(3, slot_count)
    marker_velocity = jnp.dot(
        returned, placing.T, precision=highest, preferred_element_type=jnp.float32
    )
    return (new_populations, marker_velocity)


def solution(mesh):
    return jax.shard_map(
        shards,
        mesh=mesh,
        in_specs=(
            P(None, "gx", "gy", "gz"),
            P(None, ("gx", "gy", "gz")),
            P(None, ("gx", "gy", "gz")),
            P(("gx", "gy", "gz"), None),
            P(("gx", "gy", "gz")),
        ),
        out_specs=(P(None, "gx", "gy", "gz"), P(None, ("gx", "gy", "gz"))),
        check_vma=False,
    )
```

```python
import jax
import jax.numpy as jnp
from jax import lax
from jax.sharding import PartitionSpec as P

CX = 16
CY = 16
CZ = 256
MARK_DEV = 1024


lattice_speeds = (
    (0, 0, 0),
    (1, 0, 0),
    (-1, 0, 0),
    (0, 1, 0),
    (0, -1, 0),
    (0, 0, 1),
    (0, 0, -1),
    (1, 1, 0),
    (-1, -1, 0),
    (1, -1, 0),
    (-1, 1, 0),
    (1, 0, 1),
    (-1, 0, -1),
    (1, 0, -1),
    (-1, 0, 1),
    (0, 1, 1),
    (0, -1, -1),
    (0, 1, -1),
    (0, -1, 1),
)
lattice_weights = (1.0 / 3.0,) + (1.0 / 18.0,) * 6 + (1.0 / 36.0,) * 12
relaxation = 0.8
highest = lax.Precision.HIGHEST


def extended_2(cells, sides, width):
    for axis, dim in sides:
        count = lax.axis_size(axis)
        head = lax.slice_in_dim(cells, 0, width, axis=dim)
        tail = lax.slice_in_dim(cells, cells.shape[dim] - width, cells.shape[dim], axis=dim)
        cells = jnp.concatenate(
            [
                lax.ppermute(tail, axis, [(i, (i + 1) % count) for i in range(count)]),
                cells,
                lax.ppermute(head, axis, [((i + 1) % count, i) for i in range(count)]),
            ],
            axis=dim,
        )
    return cells


def kernel_weights(offset):
    root_term = jnp.sqrt(1.0 + 4.0 * offset - 4.0 * offset * offset)
    return jnp.stack(
        [
            (3.0 - 2.0 * offset - root_term) / 8.0,
            (3.0 - 2.0 * offset + root_term) / 8.0,
            (1.0 + 2.0 * offset + root_term) / 8.0,
            (1.0 + 2.0 * offset - root_term) / 8.0,
        ]
    )


def collide(populations, forcing):
    density = jnp.sum(populations, axis=0)
    velocity = []
    for component in range(3):
        running = 0.5 * forcing[component]
        for direction in range(19):
            speed_value = lattice_speeds[direction][component]
            if speed_value != 0:
                running = running + speed_value * populations[direction]
        velocity.append(running / density)
    square = velocity[0] * velocity[0] + velocity[1] * velocity[1] + velocity[2] * velocity[2]
    collided = []
    for direction in range(19):
        speeds = lattice_speeds[direction]
        weight = lattice_weights[direction]
        contracted = jnp.zeros_like(density)
        for component in range(3):
            if speeds[component] != 0:
                contracted = contracted + speeds[component] * velocity[component]
        equilibrium = (
            weight
            * density
            * (1.0 + 3.0 * contracted + 4.5 * contracted * contracted - 1.5 * square)
        )
        source = jnp.zeros_like(density)
        for component in range(3):
            source = (
                source
                + (
                    3.0 * (speeds[component] - velocity[component])
                    + 9.0 * contracted * speeds[component]
                )
                * forcing[component]
            )
        present = populations[direction]
        collided.append(
            present
            - (present - equilibrium) / relaxation
            + (1.0 - 0.5 / relaxation) * weight * source
        )
    return (jnp.stack(collided), jnp.stack(velocity))


def fold_rims(extended, which, extent):
    middle = lax.slice_in_dim(extended, 3, extent + 3, axis=which)
    low_rims = lax.slice_in_dim(extended, 0, 2, axis=which)
    high_rims = lax.slice_in_dim(extended, extent + 5, extent + 6, axis=which)
    low_pad = [(0, 0)] * extended.ndim
    low_pad[which] = (0, extent - 2)
    high_pad = [(0, 0)] * extended.ndim
    high_pad[which] = (extent - 1, 0)
    return middle + jnp.pad(low_rims, low_pad) + jnp.pad(high_rims, high_pad)


def band_matrix(coordinate, weight, extent, anchor):
    positions = lax.broadcasted_iota(jnp.int32, (coordinate.shape[0], extent), 1)
    running = jnp.zeros((coordinate.shape[0], extent), jnp.float32)
    for shift_step in range(4):
        running = running + jnp.where(
            positions == (coordinate + anchor + shift_step)[:, None],
            weight[shift_step][:, None],
            0.0,
        )
    return running


def spread_banded(forces, coordinates, weights, grid_sizes):
    band_first = band_matrix(coordinates[0], weights[0], grid_sizes[0], 0)
    band_second = band_matrix(coordinates[1], weights[1], grid_sizes[1], 0)
    band_third = band_matrix(coordinates[2], weights[2], grid_sizes[2], 0)
    partial_value = (
        forces[:, None, None, :]
        * band_first.T[None, :, None, :]
        * band_second.T[None, None, :, :]
    )
    partial_value = partial_value.reshape(-1, forces.shape[1])
    partial_value, band_third = lax.optimization_barrier((partial_value, band_third))
    product = jnp.dot(
        partial_value, band_third, precision=highest, preferred_element_type=jnp.float32
    )
    return product.reshape((3,) + grid_sizes)


def sample_banded(velocity_ext, coordinates, weights, grid_sizes):
    flat_velocity = velocity_ext.reshape(3 * grid_sizes[0] * grid_sizes[1], grid_sizes[2])
    band_first = band_matrix(coordinates[0], weights[0], grid_sizes[0], 1)
    band_second = band_matrix(coordinates[1], weights[1], grid_sizes[1], 1)
    band_third = band_matrix(coordinates[2], weights[2], grid_sizes[2], 1)
    contracted = jnp.dot(
        flat_velocity, band_third.T, precision=highest, preferred_element_type=jnp.float32
    )
    contracted = contracted.reshape(3, grid_sizes[0], grid_sizes[1], -1)
    return jnp.sum(
        contracted * band_first.T[None, :, None, :] * band_second.T[None, None, :, :],
        axis=(1, 2),
    )


def shards(populations, marker_force, marker_offset, marker_owner, marker_cell):
    count_first = lax.axis_size("gx")
    count_rest = lax.axis_size("gy") * lax.axis_size("gz")
    devices = count_first * count_rest
    capacity = max(4, 2 * MARK_DEV // devices)
    slot_count = devices * capacity
    owners = marker_owner[:, 0]
    row_order = lax.broadcasted_iota(jnp.int32, (MARK_DEV, MARK_DEV), 0)
    column_order = lax.broadcasted_iota(jnp.int32, (MARK_DEV, MARK_DEV), 1)
    earlier = (owners[:, None] == owners[None, :]) & (column_order < row_order)
    before = jnp.sum(earlier.astype(jnp.int32), axis=1)
    slot_index = owners * capacity + before
    placing = (
        slot_index[:, None] == lax.broadcasted_iota(jnp.int32, (MARK_DEV, slot_count), 1)
    ).astype(jnp.float32)
    record = jnp.concatenate(
        [marker_offset, marker_force, marker_cell.astype(jnp.float32)[None, :]], axis=0
    )
    buckets = jnp.dot(record, placing, precision=highest, preferred_element_type=jnp.float32)
    buckets = buckets.reshape(7, count_first, count_rest, capacity)
    received = lax.all_to_all(
        lax.all_to_all(buckets, "gx", split_axis=1, concat_axis=1, tiled=True),
        ("gy", "gz"),
        split_axis=2,
        concat_axis=2,
        tiled=True,
    )
    received = received.reshape(7, slot_count)
    forces = received[3:6]
    cell_index = received[6].astype(jnp.int32)
    coordinates = (cell_index // (CY * CZ), cell_index // CZ % CY, cell_index % CZ)
    weights = (
        kernel_weights(received[0]),
        kernel_weights(received[1]),
        kernel_weights(received[2]),
    )
    ghost_sizes = (CX + 3, CY + 3, CZ + 3)
    halo_sizes = (CX + 4, CY + 4, CZ + 4)
    ghost_field = spread_banded(forces, coordinates, weights, ghost_sizes)
    force_halo = extended_2(ghost_field, (("gx", 1), ("gy", 2), ("gz", 3)), 2)
    forcing = fold_rims(fold_rims(fold_rims(force_halo, 1, CX), 2, CY), 3, CZ)
    collided, velocity = collide(populations, forcing)
    collided_ext = extended_2(collided, (("gx", 1), ("gy", 2), ("gz", 3)), 1)
    velocity_ext = extended_2(velocity, (("gx", 1), ("gy", 2), ("gz", 3)), 2)
    margin = 1
    passed = []
    for direction in range(19):
        speeds = lattice_speeds[direction]
        lower_corner = (margin - speeds[0], margin - speeds[1], margin - speeds[2])
        upper_corner = (lower_corner[0] + CX, lower_corner[1] + CY, lower_corner[2] + CZ)
        passed.append(lax.slice(collided_ext[direction], lower_corner, upper_corner))
    new_populations = jnp.stack(passed)
    sampled = sample_banded(velocity_ext, coordinates, weights, halo_sizes)
    sampled = sampled.reshape(3, count_first, count_rest, capacity)
    returned = lax.all_to_all(
        lax.all_to_all(sampled, "gx", split_axis=1, concat_axis=1, tiled=True),
        ("gy", "gz"),
        split_axis=2,
        concat_axis=2,
        tiled=True,
    )
    returned = returned.reshape(3, slot_count)
    marker_velocity = jnp.dot(
        returned, placing.T, precision=highest, preferred_element_type=jnp.float32
    )
    return (new_populations, marker_velocity)


def solution(mesh):
    return jax.shard_map(
        shards,
        mesh=mesh,
        in_specs=(
            P(None, "gx", "gy", "gz"),
            P(None, ("gx", "gy", "gz")),
            P(None, ("gx", "gy", "gz")),
            P(("gx", "gy", "gz"), None),
            P(("gx", "gy", "gz")),
        ),
        out_specs=(P(None, "gx", "gy", "gz"), P(None, ("gx", "gy", "gz"))),
        check_vma=False,
    )
```

```python
import jax
import jax.numpy as jnp
from jax import lax
from jax.sharding import PartitionSpec as P

CX = 16
CY = 16
CZ = 256
MARK_DEV = 1024


lattice_speeds = (
    (0, 0, 0),
    (1, 0, 0),
    (-1, 0, 0),
    (0, 1, 0),
    (0, -1, 0),
    (0, 0, 1),
    (0, 0, -1),
    (1, 1, 0),
    (-1, -1, 0),
    (1, -1, 0),
    (-1, 1, 0),
    (1, 0, 1),
    (-1, 0, -1),
    (1, 0, -1),
    (-1, 0, 1),
    (0, 1, 1),
    (0, -1, -1),
    (0, 1, -1),
    (0, -1, 1),
)
lattice_weights = (1.0 / 3.0,) + (1.0 / 18.0,) * 6 + (1.0 / 36.0,) * 12
relaxation = 0.8
highest = lax.Precision.HIGHEST


def extended_2(cells, sides, width):
    for axis, dim in sides:
        count = lax.axis_size(axis)
        head = lax.slice_in_dim(cells, 0, width, axis=dim)
        tail = lax.slice_in_dim(cells, cells.shape[dim] - width, cells.shape[dim], axis=dim)
        cells = jnp.concatenate(
            [
                lax.ppermute(tail, axis, [(i, (i + 1) % count) for i in range(count)]),
                cells,
                lax.ppermute(head, axis, [((i + 1) % count, i) for i in range(count)]),
            ],
            axis=dim,
        )
    return cells


def pass_axis(fields, axis, dim):
    count = lax.axis_size(axis)
    extent = fields[0].shape[dim]
    up = [i for i in range(len(fields)) if lattice_speeds[i][dim] == 1]
    down = [i for i in range(len(fields)) if lattice_speeds[i][dim] == -1]
    going_up = jnp.stack([lax.slice_in_dim(fields[i], extent - 1, extent, axis=dim) for i in up])
    going_down = jnp.stack([lax.slice_in_dim(fields[i], 0, 1, axis=dim) for i in down])
    from_low = lax.ppermute(going_up, axis, [(i, (i + 1) % count) for i in range(count)])
    from_high = lax.ppermute(going_down, axis, [((i + 1) % count, i) for i in range(count)])
    fields = list(fields)
    for k, i in enumerate(up):
        kept = lax.slice_in_dim(fields[i], 0, extent - 1, axis=dim)
        fields[i] = jnp.concatenate([from_low[k], kept], axis=dim)
    for k, i in enumerate(down):
        kept = lax.slice_in_dim(fields[i], 1, extent, axis=dim)
        fields[i] = jnp.concatenate([kept, from_high[k]], axis=dim)
    return fields


def kernel_weights(offset):
    root_term = jnp.sqrt(1.0 + 4.0 * offset - 4.0 * offset * offset)
    return jnp.stack(
        [
            (3.0 - 2.0 * offset - root_term) / 8.0,
            (3.0 - 2.0 * offset + root_term) / 8.0,
            (1.0 + 2.0 * offset + root_term) / 8.0,
            (1.0 + 2.0 * offset - root_term) / 8.0,
        ]
    )


def collide(populations, forcing):
    density = jnp.sum(populations, axis=0)
    velocity = []
    for component in range(3):
        running = 0.5 * forcing[component]
        for direction in range(19):
            speed_value = lattice_speeds[direction][component]
            if speed_value != 0:
                running = running + speed_value * populations[direction]
        velocity.append(running / density)
    square = velocity[0] * velocity[0] + velocity[1] * velocity[1] + velocity[2] * velocity[2]
    collided = []
    for direction in range(19):
        speeds = lattice_speeds[direction]
        weight = lattice_weights[direction]
        contracted = jnp.zeros_like(density)
        for component in range(3):
            if speeds[component] != 0:
                contracted = contracted + speeds[component] * velocity[component]
        equilibrium = (
            weight
            * density
            * (1.0 + 3.0 * contracted + 4.5 * contracted * contracted - 1.5 * square)
        )
        source = jnp.zeros_like(density)
        for component in range(3):
            source = (
                source
                + (
                    3.0 * (speeds[component] - velocity[component])
                    + 9.0 * contracted * speeds[component]
                )
                * forcing[component]
            )
        present = populations[direction]
        collided.append(
            present
            - (present - equilibrium) / relaxation
            + (1.0 - 0.5 / relaxation) * weight * source
        )
    return (collided, jnp.stack(velocity))


def fold_rims(extended, which, extent):
    middle = lax.slice_in_dim(extended, 3, extent + 3, axis=which)
    low_rims = lax.slice_in_dim(extended, 0, 2, axis=which)
    high_rims = lax.slice_in_dim(extended, extent + 5, extent + 6, axis=which)
    low_pad = [(0, 0)] * extended.ndim
    low_pad[which] = (0, extent - 2)
    high_pad = [(0, 0)] * extended.ndim
    high_pad[which] = (extent - 1, 0)
    return middle + jnp.pad(low_rims, low_pad) + jnp.pad(high_rims, high_pad)


def band_matrix(coordinate, weight, extent, anchor):
    positions = lax.broadcasted_iota(jnp.int32, (coordinate.shape[0], extent), 1)
    running = jnp.zeros((coordinate.shape[0], extent), jnp.float32)
    for shift_step in range(4):
        running = running + jnp.where(
            positions == (coordinate + anchor + shift_step)[:, None],
            weight[shift_step][:, None],
            0.0,
        )
    return running


def spread_banded(forces, coordinates, weights, grid_sizes):
    band_first = band_matrix(coordinates[0], weights[0], grid_sizes[0], 0)
    band_second = band_matrix(coordinates[1], weights[1], grid_sizes[1], 0)
    band_third = band_matrix(coordinates[2], weights[2], grid_sizes[2], 0)
    partial_value = (
        forces[:, None, None, :]
        * band_first.T[None, :, None, :]
        * band_second.T[None, None, :, :]
    )
    partial_value = partial_value.reshape(-1, forces.shape[1])
    partial_value, band_third = lax.optimization_barrier((partial_value, band_third))
    product = jnp.dot(
        partial_value, band_third, precision=highest, preferred_element_type=jnp.float32
    )
    return product.reshape((3,) + grid_sizes)


def sample_banded(velocity_ext, coordinates, weights, grid_sizes):
    flat_velocity = velocity_ext.reshape(3 * grid_sizes[0] * grid_sizes[1], grid_sizes[2])
    band_first = band_matrix(coordinates[0], weights[0], grid_sizes[0], 1)
    band_second = band_matrix(coordinates[1], weights[1], grid_sizes[1], 1)
    band_third = band_matrix(coordinates[2], weights[2], grid_sizes[2], 1)
    contracted = jnp.dot(
        flat_velocity, band_third.T, precision=highest, preferred_element_type=jnp.float32
    )
    contracted = contracted.reshape(3, grid_sizes[0], grid_sizes[1], -1)
    return jnp.sum(
        contracted * band_first.T[None, :, None, :] * band_second.T[None, None, :, :],
        axis=(1, 2),
    )


def shards(populations, marker_force, marker_offset, marker_owner, marker_cell):
    count_first = lax.axis_size("gx")
    count_rest = lax.axis_size("gy") * lax.axis_size("gz")
    devices = count_first * count_rest
    capacity = max(4, 2 * MARK_DEV // devices)
    slot_count = devices * capacity
    owners = marker_owner[:, 0]
    row_order = lax.broadcasted_iota(jnp.int32, (MARK_DEV, MARK_DEV), 0)
    column_order = lax.broadcasted_iota(jnp.int32, (MARK_DEV, MARK_DEV), 1)
    earlier = (owners[:, None] == owners[None, :]) & (column_order < row_order)
    before = jnp.sum(earlier.astype(jnp.int32), axis=1)
    slot_index = owners * capacity + before
    placing = (
        slot_index[:, None] == lax.broadcasted_iota(jnp.int32, (MARK_DEV, slot_count), 1)
    ).astype(jnp.float32)
    record = jnp.concatenate(
        [marker_offset, marker_force, marker_cell.astype(jnp.float32)[None, :]], axis=0
    )
    buckets = jnp.dot(record, placing, precision=highest, preferred_element_type=jnp.float32)
    buckets = buckets.reshape(7, count_first, count_rest, capacity)
    received = lax.all_to_all(
        lax.all_to_all(buckets, "gx", split_axis=1, concat_axis=1, tiled=True),
        ("gy", "gz"),
        split_axis=2,
        concat_axis=2,
        tiled=True,
    )
    received = received.reshape(7, slot_count)
    forces = received[3:6]
    cell_index = received[6].astype(jnp.int32)
    coordinates = (cell_index // (CY * CZ), cell_index // CZ % CY, cell_index % CZ)
    weights = (
        kernel_weights(received[0]),
        kernel_weights(received[1]),
        kernel_weights(received[2]),
    )
    ghost_sizes = (CX + 3, CY + 3, CZ + 3)
    halo_sizes = (CX + 4, CY + 4, CZ + 4)
    ghost_field = spread_banded(forces, coordinates, weights, ghost_sizes)
    force_halo = extended_2(ghost_field, (("gx", 1), ("gy", 2), ("gz", 3)), 2)
    forcing = fold_rims(fold_rims(fold_rims(force_halo, 1, CX), 2, CY), 3, CZ)
    collided, velocity = collide(populations, forcing)
    velocity_ext = extended_2(velocity, (("gx", 1), ("gy", 2), ("gz", 3)), 2)
    passed = collided
    for axis, dim in (("gx", 0), ("gy", 1), ("gz", 2)):
        passed = pass_axis(passed, axis, dim)
    new_populations = jnp.stack(passed)
    sampled = sample_banded(velocity_ext, coordinates, weights, halo_sizes)
    sampled = sampled.reshape(3, count_first, count_rest, capacity)
    returned = lax.all_to_all(
        lax.all_to_all(sampled, "gx", split_axis=1, concat_axis=1, tiled=True),
        ("gy", "gz"),
        split_axis=2,
        concat_axis=2,
        tiled=True,
    )
    returned = returned.reshape(3, slot_count)
    marker_velocity = jnp.dot(
        returned, placing.T, precision=highest, preferred_element_type=jnp.float32
    )
    return (new_populations, marker_velocity)


def solution(mesh):
    return jax.shard_map(
        shards,
        mesh=mesh,
        in_specs=(
            P(None, "gx", "gy", "gz"),
            P(None, ("gx", "gy", "gz")),
            P(None, ("gx", "gy", "gz")),
            P(("gx", "gy", "gz"), None),
            P(("gx", "gy", "gz")),
        ),
        out_specs=(P(None, "gx", "gy", "gz"), P(None, ("gx", "gy", "gz"))),
        check_vma=False,
    )
```

```python
import jax
import jax.numpy as jnp
from jax import lax
from jax.sharding import PartitionSpec as P

CX = 16
CY = 16
CZ = 256
MARK_DEV = 1024


lattice_speeds = (
    (0, 0, 0),
    (1, 0, 0),
    (-1, 0, 0),
    (0, 1, 0),
    (0, -1, 0),
    (0, 0, 1),
    (0, 0, -1),
    (1, 1, 0),
    (-1, -1, 0),
    (1, -1, 0),
    (-1, 1, 0),
    (1, 0, 1),
    (-1, 0, -1),
    (1, 0, -1),
    (-1, 0, 1),
    (0, 1, 1),
    (0, -1, -1),
    (0, 1, -1),
    (0, -1, 1),
)
lattice_weights = (1.0 / 3.0,) + (1.0 / 18.0,) * 6 + (1.0 / 36.0,) * 12
relaxation = 0.8
highest = lax.Precision.HIGHEST


def extended_2(cells, sides, width):
    for axis, dim in sides:
        count = lax.axis_size(axis)
        head = lax.slice_in_dim(cells, 0, width, axis=dim)
        tail = lax.slice_in_dim(cells, cells.shape[dim] - width, cells.shape[dim], axis=dim)
        cells = jnp.concatenate(
            [
                lax.ppermute(tail, axis, [(i, (i + 1) % count) for i in range(count)]),
                cells,
                lax.ppermute(head, axis, [((i + 1) % count, i) for i in range(count)]),
            ],
            axis=dim,
        )
    return cells


def exchange(axis, ups, downs):
    count = lax.axis_size(axis)

    def moved(parts, pairs):
        flat = jnp.concatenate([part.reshape(-1) for part in parts])
        flat = lax.ppermute(flat, axis, pairs)
        pieces, at = [], 0
        for part in parts:
            pieces.append(flat[at:at + part.size].reshape(part.shape))
            at += part.size
        return pieces

    from_low = moved(ups, [(i, (i + 1) % count) for i in range(count)])
    from_high = moved(downs, [((i + 1) % count, i) for i in range(count)])
    return from_low, from_high


def halo_step(fields, velocity, axis, dim, width):
    extent = fields[0].shape[dim]
    reach = velocity.shape[dim + 1]
    up = [i for i in range(len(fields)) if lattice_speeds[i][dim] == 1]
    down = [i for i in range(len(fields)) if lattice_speeds[i][dim] == -1]
    going_up = [lax.slice_in_dim(fields[i], extent - 1, extent, axis=dim) for i in up]
    going_down = [lax.slice_in_dim(fields[i], 0, 1, axis=dim) for i in down]
    going_up.append(lax.slice_in_dim(velocity, reach - width, reach, axis=dim + 1))
    going_down.append(lax.slice_in_dim(velocity, 0, width, axis=dim + 1))
    from_low, from_high = exchange(axis, going_up, going_down)
    velocity = jnp.concatenate([from_low[-1], velocity, from_high[-1]], axis=dim + 1)
    fields = list(fields)
    for k, i in enumerate(up):
        kept = lax.slice_in_dim(fields[i], 0, extent - 1, axis=dim)
        fields[i] = jnp.concatenate([from_low[k], kept], axis=dim)
    for k, i in enumerate(down):
        kept = lax.slice_in_dim(fields[i], 1, extent, axis=dim)
        fields[i] = jnp.concatenate([kept, from_high[k]], axis=dim)
    return fields, velocity


def kernel_weights(offset):
    root_term = jnp.sqrt(1.0 + 4.0 * offset - 4.0 * offset * offset)
    return jnp.stack(
        [
            (3.0 - 2.0 * offset - root_term) / 8.0,
            (3.0 - 2.0 * offset + root_term) / 8.0,
            (1.0 + 2.0 * offset + root_term) / 8.0,
            (1.0 + 2.0 * offset - root_term) / 8.0,
        ]
    )


def collide(populations, forcing):
    density = jnp.sum(populations, axis=0)
    velocity = []
    for component in range(3):
        running = 0.5 * forcing[component]
        for direction in range(19):
            speed_value = lattice_speeds[direction][component]
            if speed_value != 0:
                running = running + speed_value * populations[direction]
        velocity.append(running / density)
    square = velocity[0] * velocity[0] + velocity[1] * velocity[1] + velocity[2] * velocity[2]
    collided = []
    for direction in range(19):
        speeds = lattice_speeds[direction]
        weight = lattice_weights[direction]
        contracted = jnp.zeros_like(density)
        for component in range(3):
            if speeds[component] != 0:
                contracted = contracted + speeds[component] * velocity[component]
        equilibrium = (
            weight
            * density
            * (1.0 + 3.0 * contracted + 4.5 * contracted * contracted - 1.5 * square)
        )
        source = jnp.zeros_like(density)
        for component in range(3):
            source = (
                source
                + (
                    3.0 * (speeds[component] - velocity[component])
                    + 9.0 * contracted * speeds[component]
                )
                * forcing[component]
            )
        present = populations[direction]
        collided.append(
            present
            - (present - equilibrium) / relaxation
            + (1.0 - 0.5 / relaxation) * weight * source
        )
    return (collided, jnp.stack(velocity))


def fold_rims(extended, which, extent):
    middle = lax.slice_in_dim(extended, 3, extent + 3, axis=which)
    low_rims = lax.slice_in_dim(extended, 0, 2, axis=which)
    high_rims = lax.slice_in_dim(extended, extent + 5, extent + 6, axis=which)
    low_pad = [(0, 0)] * extended.ndim
    low_pad[which] = (0, extent - 2)
    high_pad = [(0, 0)] * extended.ndim
    high_pad[which] = (extent - 1, 0)
    return middle + jnp.pad(low_rims, low_pad) + jnp.pad(high_rims, high_pad)


def band_matrix(coordinate, weight, extent, anchor):
    positions = lax.broadcasted_iota(jnp.int32, (coordinate.shape[0], extent), 1)
    running = jnp.zeros((coordinate.shape[0], extent), jnp.float32)
    for shift_step in range(4):
        running = running + jnp.where(
            positions == (coordinate + anchor + shift_step)[:, None],
            weight[shift_step][:, None],
            0.0,
        )
    return running


def spread_banded(forces, coordinates, weights, grid_sizes):
    band_first = band_matrix(coordinates[0], weights[0], grid_sizes[0], 0)
    band_second = band_matrix(coordinates[1], weights[1], grid_sizes[1], 0)
    band_third = band_matrix(coordinates[2], weights[2], grid_sizes[2], 0)
    partial_value = (
        forces[:, None, None, :]
        * band_first.T[None, :, None, :]
        * band_second.T[None, None, :, :]
    )
    partial_value = partial_value.reshape(-1, forces.shape[1])
    partial_value, band_third = lax.optimization_barrier((partial_value, band_third))
    product = jnp.dot(
        partial_value, band_third, precision=highest, preferred_element_type=jnp.float32
    )
    return product.reshape((3,) + grid_sizes)


def sample_banded(velocity_ext, coordinates, weights, grid_sizes):
    flat_velocity = velocity_ext.reshape(3 * grid_sizes[0] * grid_sizes[1], grid_sizes[2])
    band_first = band_matrix(coordinates[0], weights[0], grid_sizes[0], 1)
    band_second = band_matrix(coordinates[1], weights[1], grid_sizes[1], 1)
    band_third = band_matrix(coordinates[2], weights[2], grid_sizes[2], 1)
    contracted = jnp.dot(
        flat_velocity, band_third.T, precision=highest, preferred_element_type=jnp.float32
    )
    contracted = contracted.reshape(3, grid_sizes[0], grid_sizes[1], -1)
    return jnp.sum(
        contracted * band_first.T[None, :, None, :] * band_second.T[None, None, :, :],
        axis=(1, 2),
    )


def shards(populations, marker_force, marker_offset, marker_owner, marker_cell):
    count_first = lax.axis_size("gx")
    count_rest = lax.axis_size("gy") * lax.axis_size("gz")
    devices = count_first * count_rest
    capacity = max(4, 2 * MARK_DEV // devices)
    slot_count = devices * capacity
    owners = marker_owner[:, 0]
    row_order = lax.broadcasted_iota(jnp.int32, (MARK_DEV, MARK_DEV), 0)
    column_order = lax.broadcasted_iota(jnp.int32, (MARK_DEV, MARK_DEV), 1)
    earlier = (owners[:, None] == owners[None, :]) & (column_order < row_order)
    before = jnp.sum(earlier.astype(jnp.int32), axis=1)
    slot_index = owners * capacity + before
    placing = (
        slot_index[:, None] == lax.broadcasted_iota(jnp.int32, (MARK_DEV, slot_count), 1)
    ).astype(jnp.float32)
    record = jnp.concatenate(
        [marker_offset, marker_force, marker_cell.astype(jnp.float32)[None, :]], axis=0
    )
    buckets = jnp.dot(record, placing, precision=highest, preferred_element_type=jnp.float32)
    buckets = buckets.reshape(7, count_first, count_rest, capacity)
    received = lax.all_to_all(
        lax.all_to_all(buckets, "gx", split_axis=1, concat_axis=1, tiled=True),
        ("gy", "gz"),
        split_axis=2,
        concat_axis=2,
        tiled=True,
    )
    received = received.reshape(7, slot_count)
    forces = received[3:6]
    cell_index = received[6].astype(jnp.int32)
    coordinates = (cell_index // (CY * CZ), cell_index // CZ % CY, cell_index % CZ)
    weights = (
        kernel_weights(received[0]),
        kernel_weights(received[1]),
        kernel_weights(received[2]),
    )
    ghost_sizes = (CX + 3, CY + 3, CZ + 3)
    halo_sizes = (CX + 4, CY + 4, CZ + 4)
    ghost_field = spread_banded(forces, coordinates, weights, ghost_sizes)
    force_halo = extended_2(ghost_field, (("gx", 1), ("gy", 2), ("gz", 3)), 2)
    forcing = fold_rims(fold_rims(fold_rims(force_halo, 1, CX), 2, CY), 3, CZ)
    collided, velocity = collide(populations, forcing)
    passed, velocity_ext = collided, velocity
    for axis, dim in (("gx", 0), ("gy", 1), ("gz", 2)):
        passed, velocity_ext = halo_step(passed, velocity_ext, axis, dim, 2)
    new_populations = jnp.stack(passed)
    sampled = sample_banded(velocity_ext, coordinates, weights, halo_sizes)
    sampled = sampled.reshape(3, count_first, count_rest, capacity)
    returned = lax.all_to_all(
        lax.all_to_all(sampled, "gx", split_axis=1, concat_axis=1, tiled=True),
        ("gy", "gz"),
        split_axis=2,
        concat_axis=2,
        tiled=True,
    )
    returned = returned.reshape(3, slot_count)
    marker_velocity = jnp.dot(
        returned, placing.T, precision=highest, preferred_element_type=jnp.float32
    )
    return (new_populations, marker_velocity)


def solution(mesh):
    return jax.shard_map(
        shards,
        mesh=mesh,
        in_specs=(
            P(None, "gx", "gy", "gz"),
            P(None, ("gx", "gy", "gz")),
            P(None, ("gx", "gy", "gz")),
            P(("gx", "gy", "gz"), None),
            P(("gx", "gy", "gz")),
        ),
        out_specs=(P(None, "gx", "gy", "gz"), P(None, ("gx", "gy", "gz"))),
        check_vma=False,
    )
```

```python
import jax
import jax.numpy as jnp
from jax import lax
from jax.sharding import PartitionSpec as P

CX = 16
CY = 16
CZ = 256
MARK_DEV = 1024


lattice_speeds = (
    (0, 0, 0),
    (1, 0, 0),
    (-1, 0, 0),
    (0, 1, 0),
    (0, -1, 0),
    (0, 0, 1),
    (0, 0, -1),
    (1, 1, 0),
    (-1, -1, 0),
    (1, -1, 0),
    (-1, 1, 0),
    (1, 0, 1),
    (-1, 0, -1),
    (1, 0, -1),
    (-1, 0, 1),
    (0, 1, 1),
    (0, -1, -1),
    (0, 1, -1),
    (0, -1, 1),
)
lattice_weights = (1.0 / 3.0,) + (1.0 / 18.0,) * 6 + (1.0 / 36.0,) * 12
relaxation = 0.8
highest = lax.Precision.HIGHEST


def extended_2(cells, sides, width):
    for axis, dim in sides:
        count = lax.axis_size(axis)
        head = lax.slice_in_dim(cells, 0, width, axis=dim)
        tail = lax.slice_in_dim(cells, cells.shape[dim] - width, cells.shape[dim], axis=dim)
        cells = jnp.concatenate(
            [
                lax.ppermute(tail, axis, [(i, (i + 1) % count) for i in range(count)]),
                cells,
                lax.ppermute(head, axis, [((i + 1) % count, i) for i in range(count)]),
            ],
            axis=dim,
        )
    return cells


def pass_axis(fields, axis, dim):
    count = lax.axis_size(axis)
    extent = fields[0].shape[dim]
    up = [i for i in range(len(fields)) if lattice_speeds[i][dim] == 1]
    down = [i for i in range(len(fields)) if lattice_speeds[i][dim] == -1]
    going_up = jnp.stack([lax.slice_in_dim(fields[i], extent - 1, extent, axis=dim) for i in up])
    going_down = jnp.stack([lax.slice_in_dim(fields[i], 0, 1, axis=dim) for i in down])
    from_low = lax.ppermute(going_up, axis, [(i, (i + 1) % count) for i in range(count)])
    from_high = lax.ppermute(going_down, axis, [((i + 1) % count, i) for i in range(count)])
    fields = list(fields)
    for k, i in enumerate(up):
        kept = lax.slice_in_dim(fields[i], 0, extent - 1, axis=dim)
        fields[i] = jnp.concatenate([from_low[k], kept], axis=dim)
    for k, i in enumerate(down):
        kept = lax.slice_in_dim(fields[i], 1, extent, axis=dim)
        fields[i] = jnp.concatenate([kept, from_high[k]], axis=dim)
    return fields


def kernel_weights(offset):
    root_term = jnp.sqrt(1.0 + 4.0 * offset - 4.0 * offset * offset)
    return jnp.stack(
        [
            (3.0 - 2.0 * offset - root_term) / 8.0,
            (3.0 - 2.0 * offset + root_term) / 8.0,
            (1.0 + 2.0 * offset + root_term) / 8.0,
            (1.0 + 2.0 * offset - root_term) / 8.0,
        ]
    )


def collide(populations, forcing):
    density = jnp.sum(populations, axis=0)
    velocity = []
    for component in range(3):
        running = 0.5 * forcing[component]
        for direction in range(19):
            speed_value = lattice_speeds[direction][component]
            if speed_value != 0:
                running = running + speed_value * populations[direction]
        velocity.append(running / density)
    square = velocity[0] * velocity[0] + velocity[1] * velocity[1] + velocity[2] * velocity[2]
    collided = []
    for direction in range(19):
        speeds = lattice_speeds[direction]
        weight = lattice_weights[direction]
        contracted = jnp.zeros_like(density)
        for component in range(3):
            if speeds[component] != 0:
                contracted = contracted + speeds[component] * velocity[component]
        equilibrium = (
            weight
            * density
            * (1.0 + 3.0 * contracted + 4.5 * contracted * contracted - 1.5 * square)
        )
        source = jnp.zeros_like(density)
        for component in range(3):
            source = (
                source
                + (
                    3.0 * (speeds[component] - velocity[component])
                    + 9.0 * contracted * speeds[component]
                )
                * forcing[component]
            )
        present = populations[direction]
        collided.append(
            present
            - (present - equilibrium) / relaxation
            + (1.0 - 0.5 / relaxation) * weight * source
        )
    return (collided, jnp.stack(velocity))


def fold_rims(extended, which, extent):
    middle = lax.slice_in_dim(extended, 3, extent + 3, axis=which)
    low_rims = lax.slice_in_dim(extended, 0, 2, axis=which)
    high_rims = lax.slice_in_dim(extended, extent + 5, extent + 6, axis=which)
    low_pad = [(0, 0)] * extended.ndim
    low_pad[which] = (0, extent - 2)
    high_pad = [(0, 0)] * extended.ndim
    high_pad[which] = (extent - 1, 0)
    return middle + jnp.pad(low_rims, low_pad) + jnp.pad(high_rims, high_pad)


def band_matrix(coordinate, weight, extent, anchor):
    positions = lax.broadcasted_iota(jnp.int32, (coordinate.shape[0], extent), 1)
    running = jnp.zeros((coordinate.shape[0], extent), jnp.float32)
    for shift_step in range(4):
        running = running + jnp.where(
            positions == (coordinate + anchor + shift_step)[:, None],
            weight[shift_step][:, None],
            0.0,
        )
    return running


def spread_banded(forces, coordinates, weights, grid_sizes):
    band_first = band_matrix(coordinates[0], weights[0], grid_sizes[0], 0)
    band_second = band_matrix(coordinates[1], weights[1], grid_sizes[1], 0)
    band_third = band_matrix(coordinates[2], weights[2], grid_sizes[2], 0)
    partial_value = (
        forces[:, None, None, :]
        * band_first.T[None, :, None, :]
        * band_second.T[None, None, :, :]
    )
    partial_value = partial_value.reshape(-1, forces.shape[1])
    partial_value, band_third = lax.optimization_barrier((partial_value, band_third))
    product = jnp.dot(
        partial_value, band_third, precision=highest, preferred_element_type=jnp.float32
    )
    return product.reshape((3,) + grid_sizes)


def sample_banded(velocity_ext, coordinates, weights, grid_sizes):
    flat_velocity = velocity_ext.reshape(3 * grid_sizes[0] * grid_sizes[1], grid_sizes[2])
    band_first = band_matrix(coordinates[0], weights[0], grid_sizes[0], 1)
    band_second = band_matrix(coordinates[1], weights[1], grid_sizes[1], 1)
    band_third = band_matrix(coordinates[2], weights[2], grid_sizes[2], 1)
    contracted = jnp.dot(
        flat_velocity, band_third.T, precision=highest, preferred_element_type=jnp.float32
    )
    contracted = contracted.reshape(3, grid_sizes[0], grid_sizes[1], -1)
    return jnp.sum(
        contracted * band_first.T[None, :, None, :] * band_second.T[None, None, :, :],
        axis=(1, 2),
    )


def shards(populations, marker_force, marker_offset, marker_owner, marker_cell):
    count_first = lax.axis_size("gx")
    count_rest = lax.axis_size("gy") * lax.axis_size("gz")
    devices = count_first * count_rest
    capacity = max(4, 2 * MARK_DEV // devices)
    slot_count = devices * capacity
    owners = marker_owner[:, 0]
    row_order = lax.broadcasted_iota(jnp.int32, (MARK_DEV, MARK_DEV), 0)
    column_order = lax.broadcasted_iota(jnp.int32, (MARK_DEV, MARK_DEV), 1)
    earlier = (owners[:, None] == owners[None, :]) & (column_order < row_order)
    before = jnp.sum(earlier.astype(jnp.int32), axis=1)
    slot_index = owners * capacity + before
    placing = (
        slot_index[:, None] == lax.broadcasted_iota(jnp.int32, (MARK_DEV, slot_count), 1)
    ).astype(jnp.float32)
    record = jnp.concatenate(
        [marker_offset, marker_force, marker_cell.astype(jnp.float32)[None, :]], axis=0
    )
    buckets = jnp.dot(record, placing, precision=highest, preferred_element_type=jnp.float32)
    everyone = ("gx", "gy", "gz")
    received = lax.all_to_all(buckets, everyone, split_axis=1, concat_axis=1, tiled=True)
    received = received.reshape(7, slot_count)
    forces = received[3:6]
    cell_index = received[6].astype(jnp.int32)
    coordinates = (cell_index // (CY * CZ), cell_index // CZ % CY, cell_index % CZ)
    weights = (
        kernel_weights(received[0]),
        kernel_weights(received[1]),
        kernel_weights(received[2]),
    )
    ghost_sizes = (CX + 3, CY + 3, CZ + 3)
    halo_sizes = (CX + 4, CY + 4, CZ + 4)
    ghost_field = spread_banded(forces, coordinates, weights, ghost_sizes)
    force_halo = extended_2(ghost_field, (("gx", 1), ("gy", 2), ("gz", 3)), 2)
    forcing = fold_rims(fold_rims(fold_rims(force_halo, 1, CX), 2, CY), 3, CZ)
    collided, velocity = collide(populations, forcing)
    velocity_ext = extended_2(velocity, (("gx", 1), ("gy", 2), ("gz", 3)), 2)
    passed = collided
    for axis, dim in (("gx", 0), ("gy", 1), ("gz", 2)):
        passed = pass_axis(passed, axis, dim)
    new_populations = jnp.stack(passed)
    sampled = sample_banded(velocity_ext, coordinates, weights, halo_sizes)
    returned = lax.all_to_all(sampled, everyone, split_axis=1, concat_axis=1, tiled=True)
    returned = returned.reshape(3, slot_count)
    marker_velocity = jnp.dot(
        returned, placing.T, precision=highest, preferred_element_type=jnp.float32
    )
    return (new_populations, marker_velocity)


def solution(mesh):
    return jax.shard_map(
        shards,
        mesh=mesh,
        in_specs=(
            P(None, "gx", "gy", "gz"),
            P(None, ("gx", "gy", "gz")),
            P(None, ("gx", "gy", "gz")),
            P(("gx", "gy", "gz"), None),
            P(("gx", "gy", "gz")),
        ),
        out_specs=(P(None, "gx", "gy", "gz"), P(None, ("gx", "gy", "gz"))),
        check_vma=False,
    )
```

```python
import jax
import jax.numpy as jnp
from jax import lax
from jax.sharding import PartitionSpec as P

CX = 16
CY = 16
CZ = 256
MARK_DEV = 1024


lattice_speeds = (
    (0, 0, 0),
    (1, 0, 0),
    (-1, 0, 0),
    (0, 1, 0),
    (0, -1, 0),
    (0, 0, 1),
    (0, 0, -1),
    (1, 1, 0),
    (-1, -1, 0),
    (1, -1, 0),
    (-1, 1, 0),
    (1, 0, 1),
    (-1, 0, -1),
    (1, 0, -1),
    (-1, 0, 1),
    (0, 1, 1),
    (0, -1, -1),
    (0, 1, -1),
    (0, -1, 1),
)
lattice_weights = (1.0 / 3.0,) + (1.0 / 18.0,) * 6 + (1.0 / 36.0,) * 12
relaxation = 0.8
highest = lax.Precision.HIGHEST
three_pass = lax.Precision.HIGH


def extended_2(cells, sides, width):
    for axis, dim in sides:
        count = lax.axis_size(axis)
        head = lax.slice_in_dim(cells, 0, width, axis=dim)
        tail = lax.slice_in_dim(cells, cells.shape[dim] - width, cells.shape[dim], axis=dim)
        cells = jnp.concatenate(
            [
                lax.ppermute(tail, axis, [(i, (i + 1) % count) for i in range(count)]),
                cells,
                lax.ppermute(head, axis, [((i + 1) % count, i) for i in range(count)]),
            ],
            axis=dim,
        )
    return cells


def pass_axis(fields, axis, dim):
    count = lax.axis_size(axis)
    extent = fields[0].shape[dim]
    up = [i for i in range(len(fields)) if lattice_speeds[i][dim] == 1]
    down = [i for i in range(len(fields)) if lattice_speeds[i][dim] == -1]
    going_up = jnp.stack([lax.slice_in_dim(fields[i], extent - 1, extent, axis=dim) for i in up])
    going_down = jnp.stack([lax.slice_in_dim(fields[i], 0, 1, axis=dim) for i in down])
    from_low = lax.ppermute(going_up, axis, [(i, (i + 1) % count) for i in range(count)])
    from_high = lax.ppermute(going_down, axis, [((i + 1) % count, i) for i in range(count)])
    fields = list(fields)
    for k, i in enumerate(up):
        kept = lax.slice_in_dim(fields[i], 0, extent - 1, axis=dim)
        fields[i] = jnp.concatenate([from_low[k], kept], axis=dim)
    for k, i in enumerate(down):
        kept = lax.slice_in_dim(fields[i], 1, extent, axis=dim)
        fields[i] = jnp.concatenate([kept, from_high[k]], axis=dim)
    return fields


def kernel_weights(offset):
    root_term = jnp.sqrt(1.0 + 4.0 * offset - 4.0 * offset * offset)
    return jnp.stack(
        [
            (3.0 - 2.0 * offset - root_term) / 8.0,
            (3.0 - 2.0 * offset + root_term) / 8.0,
            (1.0 + 2.0 * offset + root_term) / 8.0,
            (1.0 + 2.0 * offset - root_term) / 8.0,
        ]
    )


def collide(populations, forcing):
    density = jnp.sum(populations, axis=0)
    velocity = []
    for component in range(3):
        running = 0.5 * forcing[component]
        for direction in range(19):
            speed_value = lattice_speeds[direction][component]
            if speed_value != 0:
                running = running + speed_value * populations[direction]
        velocity.append(running / density)
    square = velocity[0] * velocity[0] + velocity[1] * velocity[1] + velocity[2] * velocity[2]
    collided = []
    for direction in range(19):
        speeds = lattice_speeds[direction]
        weight = lattice_weights[direction]
        contracted = jnp.zeros_like(density)
        for component in range(3):
            if speeds[component] != 0:
                contracted = contracted + speeds[component] * velocity[component]
        equilibrium = (
            weight
            * density
            * (1.0 + 3.0 * contracted + 4.5 * contracted * contracted - 1.5 * square)
        )
        source = jnp.zeros_like(density)
        for component in range(3):
            source = (
                source
                + (
                    3.0 * (speeds[component] - velocity[component])
                    + 9.0 * contracted * speeds[component]
                )
                * forcing[component]
            )
        present = populations[direction]
        collided.append(
            present
            - (present - equilibrium) / relaxation
            + (1.0 - 0.5 / relaxation) * weight * source
        )
    return (collided, jnp.stack(velocity))


def fold_rims(extended, which, extent):
    middle = lax.slice_in_dim(extended, 3, extent + 3, axis=which)
    low_rims = lax.slice_in_dim(extended, 0, 2, axis=which)
    high_rims = lax.slice_in_dim(extended, extent + 5, extent + 6, axis=which)
    low_pad = [(0, 0)] * extended.ndim
    low_pad[which] = (0, extent - 2)
    high_pad = [(0, 0)] * extended.ndim
    high_pad[which] = (extent - 1, 0)
    return middle + jnp.pad(low_rims, low_pad) + jnp.pad(high_rims, high_pad)


def band_matrix(coordinate, weight, extent, anchor):
    positions = lax.broadcasted_iota(jnp.int32, (coordinate.shape[0], extent), 1)
    running = jnp.zeros((coordinate.shape[0], extent), jnp.float32)
    for shift_step in range(4):
        running = running + jnp.where(
            positions == (coordinate + anchor + shift_step)[:, None],
            weight[shift_step][:, None],
            0.0,
        )
    return running


def spread_banded(forces, coordinates, weights, grid_sizes):
    band_first = band_matrix(coordinates[0], weights[0], grid_sizes[0], 0)
    band_second = band_matrix(coordinates[1], weights[1], grid_sizes[1], 0)
    band_third = band_matrix(coordinates[2], weights[2], grid_sizes[2], 0)
    partial_value = (
        forces[:, None, None, :]
        * band_first.T[None, :, None, :]
        * band_second.T[None, None, :, :]
    )
    partial_value = partial_value.reshape(-1, forces.shape[1])
    partial_value, band_third = lax.optimization_barrier((partial_value, band_third))
    product = jnp.dot(
        partial_value, band_third, precision=three_pass, preferred_element_type=jnp.float32
    )
    return product.reshape((3,) + grid_sizes)


def sample_banded(velocity_ext, coordinates, weights, grid_sizes):
    flat_velocity = velocity_ext.reshape(3 * grid_sizes[0] * grid_sizes[1], grid_sizes[2])
    band_first = band_matrix(coordinates[0], weights[0], grid_sizes[0], 1)
    band_second = band_matrix(coordinates[1], weights[1], grid_sizes[1], 1)
    band_third = band_matrix(coordinates[2], weights[2], grid_sizes[2], 1)
    contracted = jnp.dot(
        flat_velocity, band_third.T, precision=three_pass, preferred_element_type=jnp.float32
    )
    contracted = contracted.reshape(3, grid_sizes[0], grid_sizes[1], -1)
    return jnp.sum(
        contracted * band_first.T[None, :, None, :] * band_second.T[None, None, :, :],
        axis=(1, 2),
    )


def shards(populations, marker_force, marker_offset, marker_owner, marker_cell):
    count_first = lax.axis_size("gx")
    count_rest = lax.axis_size("gy") * lax.axis_size("gz")
    devices = count_first * count_rest
    capacity = max(4, 2 * MARK_DEV // devices)
    slot_count = devices * capacity
    owners = marker_owner[:, 0]
    row_order = lax.broadcasted_iota(jnp.int32, (MARK_DEV, MARK_DEV), 0)
    column_order = lax.broadcasted_iota(jnp.int32, (MARK_DEV, MARK_DEV), 1)
    earlier = (owners[:, None] == owners[None, :]) & (column_order < row_order)
    before = jnp.sum(earlier.astype(jnp.int32), axis=1)
    slot_index = owners * capacity + before
    placing = (
        slot_index[:, None] == lax.broadcasted_iota(jnp.int32, (MARK_DEV, slot_count), 1)
    ).astype(jnp.float32)
    record = jnp.concatenate(
        [marker_offset, marker_force, marker_cell.astype(jnp.float32)[None, :]], axis=0
    )
    buckets = jnp.dot(record, placing, precision=highest, preferred_element_type=jnp.float32)
    buckets = buckets.reshape(7, count_first, count_rest, capacity)
    received = lax.all_to_all(
        lax.all_to_all(buckets, "gx", split_axis=1, concat_axis=1, tiled=True),
        ("gy", "gz"),
        split_axis=2,
        concat_axis=2,
        tiled=True,
    )
    received = received.reshape(7, slot_count)
    forces = received[3:6]
    cell_index = received[6].astype(jnp.int32)
    coordinates = (cell_index // (CY * CZ), cell_index // CZ % CY, cell_index % CZ)
    weights = (
        kernel_weights(received[0]),
        kernel_weights(received[1]),
        kernel_weights(received[2]),
    )
    ghost_sizes = (CX + 3, CY + 3, CZ + 3)
    halo_sizes = (CX + 4, CY + 4, CZ + 4)
    ghost_field = spread_banded(forces, coordinates, weights, ghost_sizes)
    force_halo = extended_2(ghost_field, (("gx", 1), ("gy", 2), ("gz", 3)), 2)
    forcing = fold_rims(fold_rims(fold_rims(force_halo, 1, CX), 2, CY), 3, CZ)
    collided, velocity = collide(populations, forcing)
    velocity_ext = extended_2(velocity, (("gx", 1), ("gy", 2), ("gz", 3)), 2)
    passed = collided
    for axis, dim in (("gx", 0), ("gy", 1), ("gz", 2)):
        passed = pass_axis(passed, axis, dim)
    new_populations = jnp.stack(passed)
    sampled = sample_banded(velocity_ext, coordinates, weights, halo_sizes)
    sampled = sampled.reshape(3, count_first, count_rest, capacity)
    returned = lax.all_to_all(
        lax.all_to_all(sampled, "gx", split_axis=1, concat_axis=1, tiled=True),
        ("gy", "gz"),
        split_axis=2,
        concat_axis=2,
        tiled=True,
    )
    returned = returned.reshape(3, slot_count)
    marker_velocity = jnp.dot(
        returned, placing.T, precision=highest, preferred_element_type=jnp.float32
    )
    return (new_populations, marker_velocity)


def solution(mesh):
    return jax.shard_map(
        shards,
        mesh=mesh,
        in_specs=(
            P(None, "gx", "gy", "gz"),
            P(None, ("gx", "gy", "gz")),
            P(None, ("gx", "gy", "gz")),
            P(("gx", "gy", "gz"), None),
            P(("gx", "gy", "gz")),
        ),
        out_specs=(P(None, "gx", "gy", "gz"), P(None, ("gx", "gy", "gz"))),
        check_vma=False,
    )
```

```python
import jax
import jax.numpy as jnp
from jax import lax
from jax.sharding import PartitionSpec as P

CX = 16
CY = 16
CZ = 256
MARK_DEV = 1024


lattice_speeds = (
    (0, 0, 0),
    (1, 0, 0),
    (-1, 0, 0),
    (0, 1, 0),
    (0, -1, 0),
    (0, 0, 1),
    (0, 0, -1),
    (1, 1, 0),
    (-1, -1, 0),
    (1, -1, 0),
    (-1, 1, 0),
    (1, 0, 1),
    (-1, 0, -1),
    (1, 0, -1),
    (-1, 0, 1),
    (0, 1, 1),
    (0, -1, -1),
    (0, 1, -1),
    (0, -1, 1),
)
lattice_weights = (1.0 / 3.0,) + (1.0 / 18.0,) * 6 + (1.0 / 36.0,) * 12
relaxation = 0.8
highest = lax.Precision.HIGHEST
three_pass = lax.Precision.HIGH


def extended_2(cells, sides, width):
    for axis, dim in sides:
        count = lax.axis_size(axis)
        head = lax.slice_in_dim(cells, 0, width, axis=dim)
        tail = lax.slice_in_dim(cells, cells.shape[dim] - width, cells.shape[dim], axis=dim)
        cells = jnp.concatenate(
            [
                lax.ppermute(tail, axis, [(i, (i + 1) % count) for i in range(count)]),
                cells,
                lax.ppermute(head, axis, [((i + 1) % count, i) for i in range(count)]),
            ],
            axis=dim,
        )
    return cells


def pass_all(fields, axes):
    shape = fields[0].shape
    received = [dict() for _ in fields]

    def view(i, stage, ranges):
        if any(stop <= start for start, stop in ranges):
            return None
        if stage == 0:
            return fields[i][tuple(slice(start, stop) for start, stop in ranges)]
        dim = stage - 1
        speed = lattice_speeds[i][dim]
        if speed == 0:
            return view(i, stage - 1, ranges)
        start, stop = ranges[dim]
        extent = shape[dim]
        shifted = list(ranges)
        shifted[dim] = (start - speed, stop - speed)
        if speed == 1 and start == 0:
            shifted[dim] = (0, stop - 1)
            edge_at = 0
        elif speed == -1 and stop == extent:
            shifted[dim] = (start + 1, extent)
            edge_at = 1
        else:
            return view(i, stage - 1, shifted)
        edge_ranges = [(0, 1) if d == dim else ranges[d] for d in range(3)]
        edge = received[i][dim][tuple(slice(a, b) for a, b in edge_ranges)]
        rest = view(i, stage - 1, shifted)
        if rest is None:
            return edge
        parts = [edge, rest] if edge_at == 0 else [rest, edge]
        return jnp.concatenate(parts, axis=dim)

    for dim, axis in enumerate(axes):
        count = lax.axis_size(axis)
        extent = shape[dim]
        full = [(0, n) for n in shape]
        up = [i for i in range(len(fields)) if lattice_speeds[i][dim] == 1]
        down = [i for i in range(len(fields)) if lattice_speeds[i][dim] == -1]
        top = [(extent - 1, extent) if d == dim else full[d] for d in range(3)]
        bottom = [(0, 1) if d == dim else full[d] for d in range(3)]
        going_up = jnp.stack([view(i, dim, top) for i in up])
        going_down = jnp.stack([view(i, dim, bottom) for i in down])
        from_low = lax.ppermute(going_up, axis, [(j, (j + 1) % count) for j in range(count)])
        from_high = lax.ppermute(going_down, axis, [((j + 1) % count, j) for j in range(count)])
        for k, i in enumerate(up):
            received[i][dim] = from_low[k]
        for k, i in enumerate(down):
            received[i][dim] = from_high[k]
    return [view(i, 3, [(0, n) for n in shape]) for i in range(len(fields))]


def kernel_weights(offset):
    root_term = jnp.sqrt(1.0 + 4.0 * offset - 4.0 * offset * offset)
    return jnp.stack(
        [
            (3.0 - 2.0 * offset - root_term) / 8.0,
            (3.0 - 2.0 * offset + root_term) / 8.0,
            (1.0 + 2.0 * offset + root_term) / 8.0,
            (1.0 + 2.0 * offset - root_term) / 8.0,
        ]
    )


def collide(populations, forcing):
    density = jnp.sum(populations, axis=0)
    velocity = []
    for component in range(3):
        running = 0.5 * forcing[component]
        for direction in range(19):
            speed_value = lattice_speeds[direction][component]
            if speed_value != 0:
                running = running + speed_value * populations[direction]
        velocity.append(running / density)
    square = velocity[0] * velocity[0] + velocity[1] * velocity[1] + velocity[2] * velocity[2]
    collided = []
    for direction in range(19):
        speeds = lattice_speeds[direction]
        weight = lattice_weights[direction]
        contracted = jnp.zeros_like(density)
        for component in range(3):
            if speeds[component] != 0:
                contracted = contracted + speeds[component] * velocity[component]
        equilibrium = (
            weight
            * density
            * (1.0 + 3.0 * contracted + 4.5 * contracted * contracted - 1.5 * square)
        )
        source = jnp.zeros_like(density)
        for component in range(3):
            source = (
                source
                + (
                    3.0 * (speeds[component] - velocity[component])
                    + 9.0 * contracted * speeds[component]
                )
                * forcing[component]
            )
        present = populations[direction]
        collided.append(
            present
            - (present - equilibrium) / relaxation
            + (1.0 - 0.5 / relaxation) * weight * source
        )
    return (collided, jnp.stack(velocity))


def fold_rims(extended, which, extent):
    middle = lax.slice_in_dim(extended, 3, extent + 3, axis=which)
    low_rims = lax.slice_in_dim(extended, 0, 2, axis=which)
    high_rims = lax.slice_in_dim(extended, extent + 5, extent + 6, axis=which)
    low_pad = [(0, 0)] * extended.ndim
    low_pad[which] = (0, extent - 2)
    high_pad = [(0, 0)] * extended.ndim
    high_pad[which] = (extent - 1, 0)
    return middle + jnp.pad(low_rims, low_pad) + jnp.pad(high_rims, high_pad)


def band_matrix(coordinate, weight, extent, anchor):
    positions = lax.broadcasted_iota(jnp.int32, (coordinate.shape[0], extent), 1)
    running = jnp.zeros((coordinate.shape[0], extent), jnp.float32)
    for shift_step in range(4):
        running = running + jnp.where(
            positions == (coordinate + anchor + shift_step)[:, None],
            weight[shift_step][:, None],
            0.0,
        )
    return running


def spread_banded(forces, coordinates, weights, grid_sizes):
    band_first = band_matrix(coordinates[0], weights[0], grid_sizes[0], 0)
    band_second = band_matrix(coordinates[1], weights[1], grid_sizes[1], 0)
    band_third = band_matrix(coordinates[2], weights[2], grid_sizes[2], 0)
    partial_value = (
        forces[:, None, None, :]
        * band_first.T[None, :, None, :]
        * band_second.T[None, None, :, :]
    )
    partial_value = partial_value.reshape(-1, forces.shape[1])
    partial_value, band_third = lax.optimization_barrier((partial_value, band_third))
    product = jnp.dot(
        partial_value, band_third, precision=three_pass, preferred_element_type=jnp.float32
    )
    return product.reshape((3,) + grid_sizes)


def sample_banded(velocity_ext, coordinates, weights, grid_sizes):
    flat_velocity = velocity_ext.reshape(3 * grid_sizes[0] * grid_sizes[1], grid_sizes[2])
    band_first = band_matrix(coordinates[0], weights[0], grid_sizes[0], 1)
    band_second = band_matrix(coordinates[1], weights[1], grid_sizes[1], 1)
    band_third = band_matrix(coordinates[2], weights[2], grid_sizes[2], 1)
    contracted = jnp.dot(
        flat_velocity, band_third.T, precision=three_pass, preferred_element_type=jnp.float32
    )
    contracted = contracted.reshape(3, grid_sizes[0], grid_sizes[1], -1)
    return jnp.sum(
        contracted * band_first.T[None, :, None, :] * band_second.T[None, None, :, :],
        axis=(1, 2),
    )


def shards(populations, marker_force, marker_offset, marker_owner, marker_cell):
    count_first = lax.axis_size("gx")
    count_rest = lax.axis_size("gy") * lax.axis_size("gz")
    devices = count_first * count_rest
    capacity = max(4, 2 * MARK_DEV // devices)
    slot_count = devices * capacity
    owners = marker_owner[:, 0]
    row_order = lax.broadcasted_iota(jnp.int32, (MARK_DEV, MARK_DEV), 0)
    column_order = lax.broadcasted_iota(jnp.int32, (MARK_DEV, MARK_DEV), 1)
    earlier = (owners[:, None] == owners[None, :]) & (column_order < row_order)
    before = jnp.sum(earlier.astype(jnp.int32), axis=1)
    slot_index = owners * capacity + before
    placing = (
        slot_index[:, None] == lax.broadcasted_iota(jnp.int32, (MARK_DEV, slot_count), 1)
    ).astype(jnp.float32)
    record = jnp.concatenate(
        [marker_offset, marker_force, marker_cell.astype(jnp.float32)[None, :]], axis=0
    )
    buckets = jnp.dot(record, placing, precision=highest, preferred_element_type=jnp.float32)
    buckets = buckets.reshape(7, count_first, count_rest, capacity)
    received = lax.all_to_all(
        lax.all_to_all(buckets, "gx", split_axis=1, concat_axis=1, tiled=True),
        ("gy", "gz"),
        split_axis=2,
        concat_axis=2,
        tiled=True,
    )
    received = received.reshape(7, slot_count)
    forces = received[3:6]
    cell_index = received[6].astype(jnp.int32)
    coordinates = (cell_index // (CY * CZ), cell_index // CZ % CY, cell_index % CZ)
    weights = (
        kernel_weights(received[0]),
        kernel_weights(received[1]),
        kernel_weights(received[2]),
    )
    ghost_sizes = (CX + 3, CY + 3, CZ + 3)
    halo_sizes = (CX + 4, CY + 4, CZ + 4)
    ghost_field = spread_banded(forces, coordinates, weights, ghost_sizes)
    force_halo = extended_2(ghost_field, (("gx", 1), ("gy", 2), ("gz", 3)), 2)
    forcing = fold_rims(fold_rims(fold_rims(force_halo, 1, CX), 2, CY), 3, CZ)
    collided, velocity = collide(populations, forcing)
    velocity_ext = extended_2(velocity, (("gx", 1), ("gy", 2), ("gz", 3)), 2)
    new_populations = jnp.stack(pass_all(collided, ("gx", "gy", "gz")))
    sampled = sample_banded(velocity_ext, coordinates, weights, halo_sizes)
    sampled = sampled.reshape(3, count_first, count_rest, capacity)
    returned = lax.all_to_all(
        lax.all_to_all(sampled, "gx", split_axis=1, concat_axis=1, tiled=True),
        ("gy", "gz"),
        split_axis=2,
        concat_axis=2,
        tiled=True,
    )
    returned = returned.reshape(3, slot_count)
    marker_velocity = jnp.dot(
        returned, placing.T, precision=highest, preferred_element_type=jnp.float32
    )
    return (new_populations, marker_velocity)


def solution(mesh):
    return jax.shard_map(
        shards,
        mesh=mesh,
        in_specs=(
            P(None, "gx", "gy", "gz"),
            P(None, ("gx", "gy", "gz")),
            P(None, ("gx", "gy", "gz")),
            P(("gx", "gy", "gz"), None),
            P(("gx", "gy", "gz")),
        ),
        out_specs=(P(None, "gx", "gy", "gz"), P(None, ("gx", "gy", "gz"))),
        check_vma=False,
    )
```

```python
import jax
import jax.numpy as jnp
from jax import lax
from jax.sharding import PartitionSpec as P

CX = 16
CY = 16
CZ = 256
MARK_DEV = 1024


lattice_speeds = (
    (0, 0, 0),
    (1, 0, 0),
    (-1, 0, 0),
    (0, 1, 0),
    (0, -1, 0),
    (0, 0, 1),
    (0, 0, -1),
    (1, 1, 0),
    (-1, -1, 0),
    (1, -1, 0),
    (-1, 1, 0),
    (1, 0, 1),
    (-1, 0, -1),
    (1, 0, -1),
    (-1, 0, 1),
    (0, 1, 1),
    (0, -1, -1),
    (0, 1, -1),
    (0, -1, 1),
)
lattice_weights = (1.0 / 3.0,) + (1.0 / 18.0,) * 6 + (1.0 / 36.0,) * 12
relaxation = 0.8
highest = lax.Precision.HIGHEST
three_pass = lax.Precision.HIGH


def extended_2(cells, sides, width):
    for axis, dim in sides:
        count = lax.axis_size(axis)
        head = lax.slice_in_dim(cells, 0, width, axis=dim)
        tail = lax.slice_in_dim(cells, cells.shape[dim] - width, cells.shape[dim], axis=dim)
        cells = jnp.concatenate(
            [
                lax.ppermute(tail, axis, [(i, (i + 1) % count) for i in range(count)]),
                cells,
                lax.ppermute(head, axis, [((i + 1) % count, i) for i in range(count)]),
            ],
            axis=dim,
        )
    return cells


def pass_axis(fields, axis, dim):
    count = lax.axis_size(axis)
    extent = fields[0].shape[dim]
    up = [i for i in range(len(fields)) if lattice_speeds[i][dim] == 1]
    down = [i for i in range(len(fields)) if lattice_speeds[i][dim] == -1]
    going_up = jnp.stack([lax.slice_in_dim(fields[i], extent - 1, extent, axis=dim) for i in up])
    going_down = jnp.stack([lax.slice_in_dim(fields[i], 0, 1, axis=dim) for i in down])
    from_low = lax.ppermute(going_up, axis, [(i, (i + 1) % count) for i in range(count)])
    from_high = lax.ppermute(going_down, axis, [((i + 1) % count, i) for i in range(count)])
    fields = list(fields)
    for k, i in enumerate(up):
        kept = lax.slice_in_dim(fields[i], 0, extent - 1, axis=dim)
        fields[i] = jnp.concatenate([from_low[k], kept], axis=dim)
    for k, i in enumerate(down):
        kept = lax.slice_in_dim(fields[i], 1, extent, axis=dim)
        fields[i] = jnp.concatenate([kept, from_high[k]], axis=dim)
    return fields


def kernel_weights(offset):
    root_term = jnp.sqrt(1.0 + 4.0 * offset - 4.0 * offset * offset)
    return jnp.stack(
        [
            (3.0 - 2.0 * offset - root_term) / 8.0,
            (3.0 - 2.0 * offset + root_term) / 8.0,
            (1.0 + 2.0 * offset + root_term) / 8.0,
            (1.0 + 2.0 * offset - root_term) / 8.0,
        ]
    )


def collide(populations, forcing):
    density = jnp.sum(populations, axis=0)
    velocity = []
    for component in range(3):
        running = 0.5 * forcing[component]
        for direction in range(19):
            speed_value = lattice_speeds[direction][component]
            if speed_value != 0:
                running = running + speed_value * populations[direction]
        velocity.append(running / density)
    square = velocity[0] * velocity[0] + velocity[1] * velocity[1] + velocity[2] * velocity[2]
    collided = []
    for direction in range(19):
        speeds = lattice_speeds[direction]
        weight = lattice_weights[direction]
        contracted = jnp.zeros_like(density)
        for component in range(3):
            if speeds[component] != 0:
                contracted = contracted + speeds[component] * velocity[component]
        equilibrium = (
            weight
            * density
            * (1.0 + 3.0 * contracted + 4.5 * contracted * contracted - 1.5 * square)
        )
        source = jnp.zeros_like(density)
        for component in range(3):
            source = (
                source
                + (
                    3.0 * (speeds[component] - velocity[component])
                    + 9.0 * contracted * speeds[component]
                )
                * forcing[component]
            )
        present = populations[direction]
        collided.append(
            present
            - (present - equilibrium) / relaxation
            + (1.0 - 0.5 / relaxation) * weight * source
        )
    return (collided, jnp.stack(velocity))


def fold_ghost(ghost, sides, extents):
    for (axis, dim), extent in zip(sides, extents):
        count = lax.axis_size(axis)
        below = lax.slice_in_dim(ghost, 0, 1, axis=dim)
        above = lax.slice_in_dim(ghost, extent + 1, extent + 3, axis=dim)
        from_high = lax.ppermute(below, axis, [((i + 1) % count, i) for i in range(count)])
        from_low = lax.ppermute(above, axis, [(i, (i + 1) % count) for i in range(count)])
        low_pad = [(0, 0)] * ghost.ndim
        low_pad[dim] = (0, extent - 2)
        high_pad = [(0, 0)] * ghost.ndim
        high_pad[dim] = (extent - 1, 0)
        ghost = (
            lax.slice_in_dim(ghost, 1, extent + 1, axis=dim)
            + jnp.pad(from_low, low_pad)
            + jnp.pad(from_high, high_pad)
        )
    return ghost


def fold_rims(extended, which, extent):
    middle = lax.slice_in_dim(extended, 3, extent + 3, axis=which)
    low_rims = lax.slice_in_dim(extended, 0, 2, axis=which)
    high_rims = lax.slice_in_dim(extended, extent + 5, extent + 6, axis=which)
    low_pad = [(0, 0)] * extended.ndim
    low_pad[which] = (0, extent - 2)
    high_pad = [(0, 0)] * extended.ndim
    high_pad[which] = (extent - 1, 0)
    return middle + jnp.pad(low_rims, low_pad) + jnp.pad(high_rims, high_pad)


def band_matrix(coordinate, weight, extent, anchor):
    positions = lax.broadcasted_iota(jnp.int32, (coordinate.shape[0], extent), 1)
    running = jnp.zeros((coordinate.shape[0], extent), jnp.float32)
    for shift_step in range(4):
        running = running + jnp.where(
            positions == (coordinate + anchor + shift_step)[:, None],
            weight[shift_step][:, None],
            0.0,
        )
    return running


def spread_banded(forces, coordinates, weights, grid_sizes):
    band_first = band_matrix(coordinates[0], weights[0], grid_sizes[0], 0)
    band_second = band_matrix(coordinates[1], weights[1], grid_sizes[1], 0)
    band_third = band_matrix(coordinates[2], weights[2], grid_sizes[2], 0)
    partial_value = (
        forces[:, None, None, :]
        * band_first.T[None, :, None, :]
        * band_second.T[None, None, :, :]
    )
    partial_value = partial_value.reshape(-1, forces.shape[1])
    partial_value, band_third = lax.optimization_barrier((partial_value, band_third))
    product = jnp.dot(
        partial_value, band_third, precision=three_pass, preferred_element_type=jnp.float32
    )
    return product.reshape((3,) + grid_sizes)


def sample_banded(velocity_ext, coordinates, weights, grid_sizes):
    flat_velocity = velocity_ext.reshape(3 * grid_sizes[0] * grid_sizes[1], grid_sizes[2])
    band_first = band_matrix(coordinates[0], weights[0], grid_sizes[0], 1)
    band_second = band_matrix(coordinates[1], weights[1], grid_sizes[1], 1)
    band_third = band_matrix(coordinates[2], weights[2], grid_sizes[2], 1)
    contracted = jnp.dot(
        flat_velocity, band_third.T, precision=three_pass, preferred_element_type=jnp.float32
    )
    contracted = contracted.reshape(3, grid_sizes[0], grid_sizes[1], -1)
    return jnp.sum(
        contracted * band_first.T[None, :, None, :] * band_second.T[None, None, :, :],
        axis=(1, 2),
    )


def shards(populations, marker_force, marker_offset, marker_owner, marker_cell):
    count_first = lax.axis_size("gx")
    count_rest = lax.axis_size("gy") * lax.axis_size("gz")
    devices = count_first * count_rest
    capacity = max(4, 2 * MARK_DEV // devices)
    slot_count = devices * capacity
    owners = marker_owner[:, 0]
    row_order = lax.broadcasted_iota(jnp.int32, (MARK_DEV, MARK_DEV), 0)
    column_order = lax.broadcasted_iota(jnp.int32, (MARK_DEV, MARK_DEV), 1)
    earlier = (owners[:, None] == owners[None, :]) & (column_order < row_order)
    before = jnp.sum(earlier.astype(jnp.int32), axis=1)
    slot_index = owners * capacity + before
    placing = (
        slot_index[:, None] == lax.broadcasted_iota(jnp.int32, (MARK_DEV, slot_count), 1)
    ).astype(jnp.float32)
    record = jnp.concatenate(
        [marker_offset, marker_force, marker_cell.astype(jnp.float32)[None, :]], axis=0
    )
    buckets = jnp.dot(record, placing, precision=highest, preferred_element_type=jnp.float32)
    buckets = buckets.reshape(7, count_first, count_rest, capacity)
    received = lax.all_to_all(
        lax.all_to_all(buckets, "gx", split_axis=1, concat_axis=1, tiled=True),
        ("gy", "gz"),
        split_axis=2,
        concat_axis=2,
        tiled=True,
    )
    received = received.reshape(7, slot_count)
    forces = received[3:6]
    cell_index = received[6].astype(jnp.int32)
    coordinates = (cell_index // (CY * CZ), cell_index // CZ % CY, cell_index % CZ)
    weights = (
        kernel_weights(received[0]),
        kernel_weights(received[1]),
        kernel_weights(received[2]),
    )
    ghost_sizes = (CX + 3, CY + 3, CZ + 3)
    halo_sizes = (CX + 4, CY + 4, CZ + 4)
    ghost_field = spread_banded(forces, coordinates, weights, ghost_sizes)
    forcing = fold_ghost(ghost_field, (("gx", 1), ("gy", 2), ("gz", 3)), (CX, CY, CZ))
    collided, velocity = collide(populations, forcing)
    velocity_ext = extended_2(velocity, (("gx", 1), ("gy", 2), ("gz", 3)), 2)
    passed = collided
    for axis, dim in (("gx", 0), ("gy", 1), ("gz", 2)):
        passed = pass_axis(passed, axis, dim)
    new_populations = jnp.stack(passed)
    sampled = sample_banded(velocity_ext, coordinates, weights, halo_sizes)
    sampled = sampled.reshape(3, count_first, count_rest, capacity)
    returned = lax.all_to_all(
        lax.all_to_all(sampled, "gx", split_axis=1, concat_axis=1, tiled=True),
        ("gy", "gz"),
        split_axis=2,
        concat_axis=2,
        tiled=True,
    )
    returned = returned.reshape(3, slot_count)
    marker_velocity = jnp.dot(
        returned, placing.T, precision=highest, preferred_element_type=jnp.float32
    )
    return (new_populations, marker_velocity)


def solution(mesh):
    return jax.shard_map(
        shards,
        mesh=mesh,
        in_specs=(
            P(None, "gx", "gy", "gz"),
            P(None, ("gx", "gy", "gz")),
            P(None, ("gx", "gy", "gz")),
            P(("gx", "gy", "gz"), None),
            P(("gx", "gy", "gz")),
        ),
        out_specs=(P(None, "gx", "gy", "gz"), P(None, ("gx", "gy", "gz"))),
        check_vma=False,
    )
```

```python
import jax
import jax.numpy as jnp
from jax import lax
from jax.sharding import PartitionSpec as P

CX = 16
CY = 16
CZ = 256
MARK_DEV = 1024


lattice_speeds = (
    (0, 0, 0),
    (1, 0, 0),
    (-1, 0, 0),
    (0, 1, 0),
    (0, -1, 0),
    (0, 0, 1),
    (0, 0, -1),
    (1, 1, 0),
    (-1, -1, 0),
    (1, -1, 0),
    (-1, 1, 0),
    (1, 0, 1),
    (-1, 0, -1),
    (1, 0, -1),
    (-1, 0, 1),
    (0, 1, 1),
    (0, -1, -1),
    (0, 1, -1),
    (0, -1, 1),
)
lattice_weights = (1.0 / 3.0,) + (1.0 / 18.0,) * 6 + (1.0 / 36.0,) * 12
relaxation = 0.8
highest = lax.Precision.HIGHEST
three_pass = lax.Precision.HIGH


def extended(cells, sides, low, high):
    for axis, dim in sides:
        count = lax.axis_size(axis)
        head = lax.slice_in_dim(cells, 0, high, axis=dim)
        tail = lax.slice_in_dim(cells, cells.shape[dim] - low, cells.shape[dim], axis=dim)
        cells = jnp.concatenate(
            [
                lax.ppermute(tail, axis, [(i, (i + 1) % count) for i in range(count)]),
                cells,
                lax.ppermute(head, axis, [((i + 1) % count, i) for i in range(count)]),
            ],
            axis=dim,
        )
    return cells


def extended_2(cells, sides, width):
    for axis, dim in sides:
        count = lax.axis_size(axis)
        head = lax.slice_in_dim(cells, 0, width, axis=dim)
        tail = lax.slice_in_dim(cells, cells.shape[dim] - width, cells.shape[dim], axis=dim)
        cells = jnp.concatenate(
            [
                lax.ppermute(tail, axis, [(i, (i + 1) % count) for i in range(count)]),
                cells,
                lax.ppermute(head, axis, [((i + 1) % count, i) for i in range(count)]),
            ],
            axis=dim,
        )
    return cells


def pass_axis(fields, axis, dim):
    count = lax.axis_size(axis)
    extent = fields[0].shape[dim]
    up = [i for i in range(len(fields)) if lattice_speeds[i][dim] == 1]
    down = [i for i in range(len(fields)) if lattice_speeds[i][dim] == -1]
    going_up = jnp.stack([lax.slice_in_dim(fields[i], extent - 1, extent, axis=dim) for i in up])
    going_down = jnp.stack([lax.slice_in_dim(fields[i], 0, 1, axis=dim) for i in down])
    from_low = lax.ppermute(going_up, axis, [(i, (i + 1) % count) for i in range(count)])
    from_high = lax.ppermute(going_down, axis, [((i + 1) % count, i) for i in range(count)])
    fields = list(fields)
    for k, i in enumerate(up):
        kept = lax.slice_in_dim(fields[i], 0, extent - 1, axis=dim)
        fields[i] = jnp.concatenate([from_low[k], kept], axis=dim)
    for k, i in enumerate(down):
        kept = lax.slice_in_dim(fields[i], 1, extent, axis=dim)
        fields[i] = jnp.concatenate([kept, from_high[k]], axis=dim)
    return fields


def kernel_weights(offset):
    root_term = jnp.sqrt(1.0 + 4.0 * offset - 4.0 * offset * offset)
    return jnp.stack(
        [
            (3.0 - 2.0 * offset - root_term) / 8.0,
            (3.0 - 2.0 * offset + root_term) / 8.0,
            (1.0 + 2.0 * offset + root_term) / 8.0,
            (1.0 + 2.0 * offset - root_term) / 8.0,
        ]
    )


def collide(populations, forcing):
    density = jnp.sum(populations, axis=0)
    velocity = []
    for component in range(3):
        running = 0.5 * forcing[component]
        for direction in range(19):
            speed_value = lattice_speeds[direction][component]
            if speed_value != 0:
                running = running + speed_value * populations[direction]
        velocity.append(running / density)
    square = velocity[0] * velocity[0] + velocity[1] * velocity[1] + velocity[2] * velocity[2]
    collided = []
    for direction in range(19):
        speeds = lattice_speeds[direction]
        weight = lattice_weights[direction]
        contracted = jnp.zeros_like(density)
        for component in range(3):
            if speeds[component] != 0:
                contracted = contracted + speeds[component] * velocity[component]
        equilibrium = (
            weight
            * density
            * (1.0 + 3.0 * contracted + 4.5 * contracted * contracted - 1.5 * square)
        )
        source = jnp.zeros_like(density)
        for component in range(3):
            source = (
                source
                + (
                    3.0 * (speeds[component] - velocity[component])
                    + 9.0 * contracted * speeds[component]
                )
                * forcing[component]
            )
        present = populations[direction]
        collided.append(
            present
            - (present - equilibrium) / relaxation
            + (1.0 - 0.5 / relaxation) * weight * source
        )
    return (collided, jnp.stack(velocity))


def fold_ghost(ghost, sides, extents):
    for (axis, dim), extent in zip(sides, extents):
        count = lax.axis_size(axis)
        below = lax.slice_in_dim(ghost, 0, 1, axis=dim)
        above = lax.slice_in_dim(ghost, extent + 1, extent + 3, axis=dim)
        from_high = lax.ppermute(below, axis, [((i + 1) % count, i) for i in range(count)])
        from_low = lax.ppermute(above, axis, [(i, (i + 1) % count) for i in range(count)])
        low_pad = [(0, 0)] * ghost.ndim
        low_pad[dim] = (0, extent - 2)
        high_pad = [(0, 0)] * ghost.ndim
        high_pad[dim] = (extent - 1, 0)
        ghost = (
            lax.slice_in_dim(ghost, 1, extent + 1, axis=dim)
            + jnp.pad(from_low, low_pad)
            + jnp.pad(from_high, high_pad)
        )
    return ghost


def fold_rims(extended, which, extent):
    middle = lax.slice_in_dim(extended, 3, extent + 3, axis=which)
    low_rims = lax.slice_in_dim(extended, 0, 2, axis=which)
    high_rims = lax.slice_in_dim(extended, extent + 5, extent + 6, axis=which)
    low_pad = [(0, 0)] * extended.ndim
    low_pad[which] = (0, extent - 2)
    high_pad = [(0, 0)] * extended.ndim
    high_pad[which] = (extent - 1, 0)
    return middle + jnp.pad(low_rims, low_pad) + jnp.pad(high_rims, high_pad)


def band_matrix(coordinate, weight, extent, anchor):
    positions = lax.broadcasted_iota(jnp.int32, (coordinate.shape[0], extent), 1)
    running = jnp.zeros((coordinate.shape[0], extent), jnp.float32)
    for shift_step in range(4):
        running = running + jnp.where(
            positions == (coordinate + anchor + shift_step)[:, None],
            weight[shift_step][:, None],
            0.0,
        )
    return running


def spread_banded(forces, coordinates, weights, grid_sizes):
    band_first = band_matrix(coordinates[0], weights[0], grid_sizes[0], 0)
    band_second = band_matrix(coordinates[1], weights[1], grid_sizes[1], 0)
    band_third = band_matrix(coordinates[2], weights[2], grid_sizes[2], 0)
    partial_value = (
        forces[:, None, None, :]
        * band_first.T[None, :, None, :]
        * band_second.T[None, None, :, :]
    )
    partial_value = partial_value.reshape(-1, forces.shape[1])
    partial_value, band_third = lax.optimization_barrier((partial_value, band_third))
    product = jnp.dot(
        partial_value, band_third, precision=three_pass, preferred_element_type=jnp.float32
    )
    return product.reshape((3,) + grid_sizes)


def sample_banded(velocity_ext, coordinates, weights, grid_sizes, anchor):
    flat_velocity = velocity_ext.reshape(3 * grid_sizes[0] * grid_sizes[1], grid_sizes[2])
    band_first = band_matrix(coordinates[0], weights[0], grid_sizes[0], anchor)
    band_second = band_matrix(coordinates[1], weights[1], grid_sizes[1], anchor)
    band_third = band_matrix(coordinates[2], weights[2], grid_sizes[2], anchor)
    contracted = jnp.dot(
        flat_velocity, band_third.T, precision=three_pass, preferred_element_type=jnp.float32
    )
    contracted = contracted.reshape(3, grid_sizes[0], grid_sizes[1], -1)
    return jnp.sum(
        contracted * band_first.T[None, :, None, :] * band_second.T[None, None, :, :],
        axis=(1, 2),
    )


def shards(populations, marker_force, marker_offset, marker_owner, marker_cell):
    count_first = lax.axis_size("gx")
    count_rest = lax.axis_size("gy") * lax.axis_size("gz")
    devices = count_first * count_rest
    capacity = max(4, 2 * MARK_DEV // devices)
    slot_count = devices * capacity
    owners = marker_owner[:, 0]
    row_order = lax.broadcasted_iota(jnp.int32, (MARK_DEV, MARK_DEV), 0)
    column_order = lax.broadcasted_iota(jnp.int32, (MARK_DEV, MARK_DEV), 1)
    earlier = (owners[:, None] == owners[None, :]) & (column_order < row_order)
    before = jnp.sum(earlier.astype(jnp.int32), axis=1)
    slot_index = owners * capacity + before
    placing = (
        slot_index[:, None] == lax.broadcasted_iota(jnp.int32, (MARK_DEV, slot_count), 1)
    ).astype(jnp.float32)
    record = jnp.concatenate(
        [marker_offset, marker_force, marker_cell.astype(jnp.float32)[None, :]], axis=0
    )
    buckets = jnp.dot(record, placing, precision=highest, preferred_element_type=jnp.float32)
    buckets = buckets.reshape(7, count_first, count_rest, capacity)
    received = lax.all_to_all(
        lax.all_to_all(buckets, "gx", split_axis=1, concat_axis=1, tiled=True),
        ("gy", "gz"),
        split_axis=2,
        concat_axis=2,
        tiled=True,
    )
    received = received.reshape(7, slot_count)
    forces = received[3:6]
    cell_index = received[6].astype(jnp.int32)
    coordinates = (cell_index // (CY * CZ), cell_index // CZ % CY, cell_index % CZ)
    weights = (
        kernel_weights(received[0]),
        kernel_weights(received[1]),
        kernel_weights(received[2]),
    )
    ghost_sizes = (CX + 3, CY + 3, CZ + 3)
    ghost_field = spread_banded(forces, coordinates, weights, ghost_sizes)
    forcing = fold_ghost(ghost_field, (("gx", 1), ("gy", 2), ("gz", 3)), (CX, CY, CZ))
    collided, velocity = collide(populations, forcing)
    velocity_ext = extended(velocity, (("gx", 1), ("gy", 2), ("gz", 3)), 1, 2)
    passed = collided
    for axis, dim in (("gx", 0), ("gy", 1), ("gz", 2)):
        passed = pass_axis(passed, axis, dim)
    new_populations = jnp.stack(passed)
    sampled = sample_banded(velocity_ext, coordinates, weights, ghost_sizes, 0)
    sampled = sampled.reshape(3, count_first, count_rest, capacity)
    returned = lax.all_to_all(
        lax.all_to_all(sampled, "gx", split_axis=1, concat_axis=1, tiled=True),
        ("gy", "gz"),
        split_axis=2,
        concat_axis=2,
        tiled=True,
    )
    returned = returned.reshape(3, slot_count)
    marker_velocity = jnp.dot(
        returned, placing.T, precision=highest, preferred_element_type=jnp.float32
    )
    return (new_populations, marker_velocity)


def solution(mesh):
    return jax.shard_map(
        shards,
        mesh=mesh,
        in_specs=(
            P(None, "gx", "gy", "gz"),
            P(None, ("gx", "gy", "gz")),
            P(None, ("gx", "gy", "gz")),
            P(("gx", "gy", "gz"), None),
            P(("gx", "gy", "gz")),
        ),
        out_specs=(P(None, "gx", "gy", "gz"), P(None, ("gx", "gy", "gz"))),
        check_vma=False,
    )
```

```python
import jax
import jax.numpy as jnp
from jax import lax
from jax.sharding import PartitionSpec as P

CX = 16
CY = 16
CZ = 256
MARK_DEV = 1024


lattice_speeds = (
    (0, 0, 0),
    (1, 0, 0),
    (-1, 0, 0),
    (0, 1, 0),
    (0, -1, 0),
    (0, 0, 1),
    (0, 0, -1),
    (1, 1, 0),
    (-1, -1, 0),
    (1, -1, 0),
    (-1, 1, 0),
    (1, 0, 1),
    (-1, 0, -1),
    (1, 0, -1),
    (-1, 0, 1),
    (0, 1, 1),
    (0, -1, -1),
    (0, 1, -1),
    (0, -1, 1),
)
lattice_weights = (1.0 / 3.0,) + (1.0 / 18.0,) * 6 + (1.0 / 36.0,) * 12
relaxation = 0.8
highest = lax.Precision.HIGHEST
three_pass = lax.Precision.HIGH


def extended_2(cells, sides, width):
    for axis, dim in sides:
        count = lax.axis_size(axis)
        head = lax.slice_in_dim(cells, 0, width, axis=dim)
        tail = lax.slice_in_dim(cells, cells.shape[dim] - width, cells.shape[dim], axis=dim)
        cells = jnp.concatenate(
            [
                lax.ppermute(tail, axis, [(i, (i + 1) % count) for i in range(count)]),
                cells,
                lax.ppermute(head, axis, [((i + 1) % count, i) for i in range(count)]),
            ],
            axis=dim,
        )
    return cells


def pass_axis(fields, axis, dim):
    count = lax.axis_size(axis)
    extent = fields[0].shape[dim]
    up = [i for i in range(len(fields)) if lattice_speeds[i][dim] == 1]
    down = [i for i in range(len(fields)) if lattice_speeds[i][dim] == -1]
    going_up = jnp.stack([lax.slice_in_dim(fields[i], extent - 1, extent, axis=dim) for i in up])
    going_down = jnp.stack([lax.slice_in_dim(fields[i], 0, 1, axis=dim) for i in down])
    from_low = lax.ppermute(going_up, axis, [(i, (i + 1) % count) for i in range(count)])
    from_high = lax.ppermute(going_down, axis, [((i + 1) % count, i) for i in range(count)])
    fields = list(fields)
    for k, i in enumerate(up):
        kept = lax.slice_in_dim(fields[i], 0, extent - 1, axis=dim)
        fields[i] = jnp.concatenate([from_low[k], kept], axis=dim)
    for k, i in enumerate(down):
        kept = lax.slice_in_dim(fields[i], 1, extent, axis=dim)
        fields[i] = jnp.concatenate([kept, from_high[k]], axis=dim)
    return fields


def kernel_weights(offset):
    root_term = jnp.sqrt(1.0 + 4.0 * offset - 4.0 * offset * offset)
    return jnp.stack(
        [
            (3.0 - 2.0 * offset - root_term) / 8.0,
            (3.0 - 2.0 * offset + root_term) / 8.0,
            (1.0 + 2.0 * offset + root_term) / 8.0,
            (1.0 + 2.0 * offset - root_term) / 8.0,
        ]
    )


def collide(populations, forcing):
    density = jnp.sum(populations, axis=0)
    velocity = []
    for component in range(3):
        running = 0.5 * forcing[component]
        for direction in range(19):
            speed_value = lattice_speeds[direction][component]
            if speed_value != 0:
                running = running + speed_value * populations[direction]
        velocity.append(running / density)
    square = velocity[0] * velocity[0] + velocity[1] * velocity[1] + velocity[2] * velocity[2]
    collided = []
    for direction in range(19):
        speeds = lattice_speeds[direction]
        weight = lattice_weights[direction]
        contracted = jnp.zeros_like(density)
        for component in range(3):
            if speeds[component] != 0:
                contracted = contracted + speeds[component] * velocity[component]
        equilibrium = (
            weight
            * density
            * (1.0 + 3.0 * contracted + 4.5 * contracted * contracted - 1.5 * square)
        )
        source = jnp.zeros_like(density)
        for component in range(3):
            source = (
                source
                + (
                    3.0 * (speeds[component] - velocity[component])
                    + 9.0 * contracted * speeds[component]
                )
                * forcing[component]
            )
        present = populations[direction]
        collided.append(
            present
            - (present - equilibrium) / relaxation
            + (1.0 - 0.5 / relaxation) * weight * source
        )
    return (collided, jnp.stack(velocity))


def fold_ghost(ghost, sides, extents):
    for (axis, dim), extent in zip(sides, extents):
        count = lax.axis_size(axis)
        below = lax.slice_in_dim(ghost, 0, 1, axis=dim)
        above = lax.slice_in_dim(ghost, extent + 1, extent + 3, axis=dim)
        from_high = lax.ppermute(below, axis, [((i + 1) % count, i) for i in range(count)])
        from_low = lax.ppermute(above, axis, [(i, (i + 1) % count) for i in range(count)])
        low_pad = [(0, 0)] * ghost.ndim
        low_pad[dim] = (0, extent - 2)
        high_pad = [(0, 0)] * ghost.ndim
        high_pad[dim] = (extent - 1, 0)
        ghost = (
            lax.slice_in_dim(ghost, 1, extent + 1, axis=dim)
            + jnp.pad(from_low, low_pad)
            + jnp.pad(from_high, high_pad)
        )
    return ghost


def fold_rims(extended, which, extent):
    middle = lax.slice_in_dim(extended, 3, extent + 3, axis=which)
    low_rims = lax.slice_in_dim(extended, 0, 2, axis=which)
    high_rims = lax.slice_in_dim(extended, extent + 5, extent + 6, axis=which)
    low_pad = [(0, 0)] * extended.ndim
    low_pad[which] = (0, extent - 2)
    high_pad = [(0, 0)] * extended.ndim
    high_pad[which] = (extent - 1, 0)
    return middle + jnp.pad(low_rims, low_pad) + jnp.pad(high_rims, high_pad)


def band_matrix(coordinate, weight, extent, anchor):
    positions = lax.broadcasted_iota(jnp.int32, (coordinate.shape[0], extent), 1)
    running = jnp.zeros((coordinate.shape[0], extent), jnp.float32)
    for shift_step in range(4):
        running = running + jnp.where(
            positions == (coordinate + anchor + shift_step)[:, None],
            weight[shift_step][:, None],
            0.0,
        )
    return running


def spread_banded(forces, coordinates, weights, grid_sizes):
    band_first = band_matrix(coordinates[0], weights[0], grid_sizes[0], 0)
    band_second = band_matrix(coordinates[1], weights[1], grid_sizes[1], 0)
    band_third = band_matrix(coordinates[2], weights[2], grid_sizes[2], 0)
    partial_value = (
        forces[:, None, None, :]
        * band_first.T[None, :, None, :]
        * band_second.T[None, None, :, :]
    )
    partial_value = partial_value.reshape(-1, forces.shape[1])
    partial_value, band_third = lax.optimization_barrier((partial_value, band_third))
    product = jnp.dot(
        partial_value, band_third, precision=three_pass, preferred_element_type=jnp.float32
    )
    return product.reshape((3,) + grid_sizes)


def sample_banded(velocity_ext, coordinates, weights, grid_sizes):
    flat_velocity = velocity_ext.reshape(3 * grid_sizes[0] * grid_sizes[1], grid_sizes[2])
    band_first = band_matrix(coordinates[0], weights[0], grid_sizes[0], 1)
    band_second = band_matrix(coordinates[1], weights[1], grid_sizes[1], 1)
    band_third = band_matrix(coordinates[2], weights[2], grid_sizes[2], 1)
    contracted = jnp.dot(
        flat_velocity, band_third.T, precision=three_pass, preferred_element_type=jnp.float32
    )
    contracted = contracted.reshape(3, grid_sizes[0], grid_sizes[1], -1)
    return jnp.sum(
        contracted * band_first.T[None, :, None, :] * band_second.T[None, None, :, :],
        axis=(1, 2),
    )


def shards(populations, marker_force, marker_offset, marker_owner, marker_cell):
    count_first = lax.axis_size("gx")
    count_rest = lax.axis_size("gy") * lax.axis_size("gz")
    devices = count_first * count_rest
    capacity = max(4, 2 * MARK_DEV // devices)
    slot_count = devices * capacity
    owners = marker_owner[:, 0]
    row_order = lax.broadcasted_iota(jnp.int32, (MARK_DEV, MARK_DEV), 0)
    column_order = lax.broadcasted_iota(jnp.int32, (MARK_DEV, MARK_DEV), 1)
    earlier = (owners[:, None] == owners[None, :]) & (column_order < row_order)
    before = jnp.sum(earlier.astype(jnp.int32), axis=1)
    slot_index = owners * capacity + before
    placing = (
        slot_index[:, None] == lax.broadcasted_iota(jnp.int32, (MARK_DEV, slot_count), 1)
    ).astype(jnp.float32)
    record = jnp.concatenate(
        [marker_offset, marker_force, marker_cell.astype(jnp.float32)[None, :]], axis=0
    )
    buckets = jnp.dot(record, placing, precision=highest, preferred_element_type=jnp.float32)
    buckets = buckets.reshape(7, count_first, count_rest, capacity)
    received = lax.all_to_all(
        lax.all_to_all(buckets, ("gy", "gz"), split_axis=2, concat_axis=2, tiled=True),
        "gx",
        split_axis=1,
        concat_axis=1,
        tiled=True,
    )
    received = received.reshape(7, slot_count)
    forces = received[3:6]
    cell_index = received[6].astype(jnp.int32)
    coordinates = (cell_index // (CY * CZ), cell_index // CZ % CY, cell_index % CZ)
    weights = (
        kernel_weights(received[0]),
        kernel_weights(received[1]),
        kernel_weights(received[2]),
    )
    ghost_sizes = (CX + 3, CY + 3, CZ + 3)
    halo_sizes = (CX + 4, CY + 4, CZ + 4)
    ghost_field = spread_banded(forces, coordinates, weights, ghost_sizes)
    forcing = fold_ghost(ghost_field, (("gx", 1), ("gy", 2), ("gz", 3)), (CX, CY, CZ))
    collided, velocity = collide(populations, forcing)
    velocity_ext = extended_2(velocity, (("gx", 1), ("gy", 2), ("gz", 3)), 2)
    passed = collided
    for axis, dim in (("gx", 0), ("gy", 1), ("gz", 2)):
        passed = pass_axis(passed, axis, dim)
    new_populations = jnp.stack(passed)
    sampled = sample_banded(velocity_ext, coordinates, weights, halo_sizes)
    sampled = sampled.reshape(3, count_first, count_rest, capacity)
    returned = lax.all_to_all(
        lax.all_to_all(sampled, ("gy", "gz"), split_axis=2, concat_axis=2, tiled=True),
        "gx",
        split_axis=1,
        concat_axis=1,
        tiled=True,
    )
    returned = returned.reshape(3, slot_count)
    marker_velocity = jnp.dot(
        returned, placing.T, precision=highest, preferred_element_type=jnp.float32
    )
    return (new_populations, marker_velocity)


def solution(mesh):
    return jax.shard_map(
        shards,
        mesh=mesh,
        in_specs=(
            P(None, "gx", "gy", "gz"),
            P(None, ("gx", "gy", "gz")),
            P(None, ("gx", "gy", "gz")),
            P(("gx", "gy", "gz"), None),
            P(("gx", "gy", "gz")),
        ),
        out_specs=(P(None, "gx", "gy", "gz"), P(None, ("gx", "gy", "gz"))),
        check_vma=False,
    )
```

```python
import jax
import jax.numpy as jnp
from jax import lax
from jax.sharding import PartitionSpec as P

CX = 16
CY = 16
CZ = 256
MARK_DEV = 1024


lattice_speeds = (
    (0, 0, 0),
    (1, 0, 0),
    (-1, 0, 0),
    (0, 1, 0),
    (0, -1, 0),
    (0, 0, 1),
    (0, 0, -1),
    (1, 1, 0),
    (-1, -1, 0),
    (1, -1, 0),
    (-1, 1, 0),
    (1, 0, 1),
    (-1, 0, -1),
    (1, 0, -1),
    (-1, 0, 1),
    (0, 1, 1),
    (0, -1, -1),
    (0, 1, -1),
    (0, -1, 1),
)
lattice_weights = (1.0 / 3.0,) + (1.0 / 18.0,) * 6 + (1.0 / 36.0,) * 12
relaxation = 0.8
highest = lax.Precision.HIGHEST
three_pass = lax.Precision.HIGH


def extended_2(cells, sides, width):
    for axis, dim in sides:
        count = lax.axis_size(axis)
        head = lax.slice_in_dim(cells, 0, width, axis=dim)
        tail = lax.slice_in_dim(cells, cells.shape[dim] - width, cells.shape[dim], axis=dim)
        cells = jnp.concatenate(
            [
                lax.ppermute(tail, axis, [(i, (i + 1) % count) for i in range(count)]),
                cells,
                lax.ppermute(head, axis, [((i + 1) % count, i) for i in range(count)]),
            ],
            axis=dim,
        )
    return cells


def pass_axis(fields, axis, dim):
    count = lax.axis_size(axis)
    extent = fields[0].shape[dim]
    up = [i for i in range(len(fields)) if lattice_speeds[i][dim] == 1]
    down = [i for i in range(len(fields)) if lattice_speeds[i][dim] == -1]
    going_up = jnp.stack([lax.slice_in_dim(fields[i], extent - 1, extent, axis=dim) for i in up])
    going_down = jnp.stack([lax.slice_in_dim(fields[i], 0, 1, axis=dim) for i in down])
    from_low = lax.ppermute(going_up, axis, [(i, (i + 1) % count) for i in range(count)])
    from_high = lax.ppermute(going_down, axis, [((i + 1) % count, i) for i in range(count)])
    fields = list(fields)
    for k, i in enumerate(up):
        kept = lax.slice_in_dim(fields[i], 0, extent - 1, axis=dim)
        fields[i] = jnp.concatenate([from_low[k], kept], axis=dim)
    for k, i in enumerate(down):
        kept = lax.slice_in_dim(fields[i], 1, extent, axis=dim)
        fields[i] = jnp.concatenate([kept, from_high[k]], axis=dim)
    return fields


def kernel_weights(offset):
    root_term = jnp.sqrt(1.0 + 4.0 * offset - 4.0 * offset * offset)
    return jnp.stack(
        [
            (3.0 - 2.0 * offset - root_term) / 8.0,
            (3.0 - 2.0 * offset + root_term) / 8.0,
            (1.0 + 2.0 * offset + root_term) / 8.0,
            (1.0 + 2.0 * offset - root_term) / 8.0,
        ]
    )


def collide(populations, forcing):
    density = jnp.sum(populations, axis=0)
    velocity = []
    for component in range(3):
        running = 0.5 * forcing[component]
        for direction in range(19):
            speed_value = lattice_speeds[direction][component]
            if speed_value != 0:
                running = running + speed_value * populations[direction]
        velocity.append(running / density)
    square = velocity[0] * velocity[0] + velocity[1] * velocity[1] + velocity[2] * velocity[2]
    collided = []
    for direction in range(19):
        speeds = lattice_speeds[direction]
        weight = lattice_weights[direction]
        contracted = jnp.zeros_like(density)
        for component in range(3):
            if speeds[component] != 0:
                contracted = contracted + speeds[component] * velocity[component]
        equilibrium = (
            weight
            * density
            * (1.0 + 3.0 * contracted + 4.5 * contracted * contracted - 1.5 * square)
        )
        source = jnp.zeros_like(density)
        for component in range(3):
            source = (
                source
                + (
                    3.0 * (speeds[component] - velocity[component])
                    + 9.0 * contracted * speeds[component]
                )
                * forcing[component]
            )
        present = populations[direction]
        collided.append(
            present
            - (present - equilibrium) / relaxation
            + (1.0 - 0.5 / relaxation) * weight * source
        )
    return (collided, jnp.stack(velocity))


def fold_ghost(ghost, sides, extents):
    for (axis, dim), extent in zip(sides, extents):
        count = lax.axis_size(axis)
        below = lax.slice_in_dim(ghost, 0, 1, axis=dim)
        above = lax.slice_in_dim(ghost, extent + 1, extent + 3, axis=dim)
        from_high = lax.ppermute(below, axis, [((i + 1) % count, i) for i in range(count)])
        from_low = lax.ppermute(above, axis, [(i, (i + 1) % count) for i in range(count)])
        low_pad = [(0, 0)] * ghost.ndim
        low_pad[dim] = (0, extent - 2)
        high_pad = [(0, 0)] * ghost.ndim
        high_pad[dim] = (extent - 1, 0)
        ghost = (
            lax.slice_in_dim(ghost, 1, extent + 1, axis=dim)
            + jnp.pad(from_low, low_pad)
            + jnp.pad(from_high, high_pad)
        )
    return ghost


def fold_rims(extended, which, extent):
    middle = lax.slice_in_dim(extended, 3, extent + 3, axis=which)
    low_rims = lax.slice_in_dim(extended, 0, 2, axis=which)
    high_rims = lax.slice_in_dim(extended, extent + 5, extent + 6, axis=which)
    low_pad = [(0, 0)] * extended.ndim
    low_pad[which] = (0, extent - 2)
    high_pad = [(0, 0)] * extended.ndim
    high_pad[which] = (extent - 1, 0)
    return middle + jnp.pad(low_rims, low_pad) + jnp.pad(high_rims, high_pad)


def band_matrix(coordinate, weight, extent, anchor):
    positions = lax.broadcasted_iota(jnp.int32, (coordinate.shape[0], extent), 1)
    running = jnp.zeros((coordinate.shape[0], extent), jnp.float32)
    for shift_step in range(4):
        running = running + jnp.where(
            positions == (coordinate + anchor + shift_step)[:, None],
            weight[shift_step][:, None],
            0.0,
        )
    return running


def spread_banded(forces, coordinates, weights, grid_sizes):
    band_first = band_matrix(coordinates[0], weights[0], grid_sizes[0], 0)
    band_second = band_matrix(coordinates[1], weights[1], grid_sizes[1], 0)
    band_third = band_matrix(coordinates[2], weights[2], grid_sizes[2], 0)
    slots = forces.shape[1]
    plane = (band_first[:, :, None] * band_second[:, None, :]).reshape(slots, -1)
    line = (forces.T[:, :, None] * band_third[:, None, :]).reshape(slots, -1)
    plane, line = lax.optimization_barrier((plane, line))
    product = lax.dot_general(
        plane,
        line,
        (((0,), (0,)), ((), ())),
        precision=three_pass,
        preferred_element_type=jnp.float32,
    )
    product = product.reshape(grid_sizes[0], grid_sizes[1], 3, grid_sizes[2])
    return jnp.transpose(product, (2, 0, 1, 3))


def sample_banded(velocity_ext, coordinates, weights, grid_sizes):
    flat_velocity = velocity_ext.reshape(3 * grid_sizes[0] * grid_sizes[1], grid_sizes[2])
    band_first = band_matrix(coordinates[0], weights[0], grid_sizes[0], 1)
    band_second = band_matrix(coordinates[1], weights[1], grid_sizes[1], 1)
    band_third = band_matrix(coordinates[2], weights[2], grid_sizes[2], 1)
    contracted = jnp.dot(
        flat_velocity, band_third.T, precision=three_pass, preferred_element_type=jnp.float32
    )
    contracted = contracted.reshape(3, grid_sizes[0], grid_sizes[1], -1)
    return jnp.sum(
        contracted * band_first.T[None, :, None, :] * band_second.T[None, None, :, :],
        axis=(1, 2),
    )


def shards(populations, marker_force, marker_offset, marker_owner, marker_cell):
    count_first = lax.axis_size("gx")
    count_rest = lax.axis_size("gy") * lax.axis_size("gz")
    devices = count_first * count_rest
    capacity = max(4, 2 * MARK_DEV // devices)
    slot_count = devices * capacity
    owners = marker_owner[:, 0]
    row_order = lax.broadcasted_iota(jnp.int32, (MARK_DEV, MARK_DEV), 0)
    column_order = lax.broadcasted_iota(jnp.int32, (MARK_DEV, MARK_DEV), 1)
    earlier = (owners[:, None] == owners[None, :]) & (column_order < row_order)
    before = jnp.sum(earlier.astype(jnp.int32), axis=1)
    slot_index = owners * capacity + before
    placing = (
        slot_index[:, None] == lax.broadcasted_iota(jnp.int32, (MARK_DEV, slot_count), 1)
    ).astype(jnp.float32)
    record = jnp.concatenate(
        [marker_offset, marker_force, marker_cell.astype(jnp.float32)[None, :]], axis=0
    )
    buckets = jnp.dot(record, placing, precision=highest, preferred_element_type=jnp.float32)
    buckets = buckets.reshape(7, count_first, count_rest, capacity)
    received = lax.all_to_all(
        lax.all_to_all(buckets, ("gy", "gz"), split_axis=2, concat_axis=2, tiled=True),
        "gx",
        split_axis=1,
        concat_axis=1,
        tiled=True,
    )
    received = received.reshape(7, slot_count)
    forces = received[3:6]
    cell_index = received[6].astype(jnp.int32)
    coordinates = (cell_index // (CY * CZ), cell_index // CZ % CY, cell_index % CZ)
    weights = (
        kernel_weights(received[0]),
        kernel_weights(received[1]),
        kernel_weights(received[2]),
    )
    ghost_sizes = (CX + 3, CY + 3, CZ + 3)
    halo_sizes = (CX + 4, CY + 4, CZ + 4)
    ghost_field = spread_banded(forces, coordinates, weights, ghost_sizes)
    forcing = fold_ghost(ghost_field, (("gx", 1), ("gy", 2), ("gz", 3)), (CX, CY, CZ))
    collided, velocity = collide(populations, forcing)
    velocity_ext = extended_2(velocity, (("gx", 1), ("gy", 2), ("gz", 3)), 2)
    passed = collided
    for axis, dim in (("gx", 0), ("gy", 1), ("gz", 2)):
        passed = pass_axis(passed, axis, dim)
    new_populations = jnp.stack(passed)
    sampled = sample_banded(velocity_ext, coordinates, weights, halo_sizes)
    sampled = sampled.reshape(3, count_first, count_rest, capacity)
    returned = lax.all_to_all(
        lax.all_to_all(sampled, ("gy", "gz"), split_axis=2, concat_axis=2, tiled=True),
        "gx",
        split_axis=1,
        concat_axis=1,
        tiled=True,
    )
    returned = returned.reshape(3, slot_count)
    marker_velocity = jnp.dot(
        returned, placing.T, precision=highest, preferred_element_type=jnp.float32
    )
    return (new_populations, marker_velocity)


def solution(mesh):
    return jax.shard_map(
        shards,
        mesh=mesh,
        in_specs=(
            P(None, "gx", "gy", "gz"),
            P(None, ("gx", "gy", "gz")),
            P(None, ("gx", "gy", "gz")),
            P(("gx", "gy", "gz"), None),
            P(("gx", "gy", "gz")),
        ),
        out_specs=(P(None, "gx", "gy", "gz"), P(None, ("gx", "gy", "gz"))),
        check_vma=False,
    )
```

```python
import jax
import jax.numpy as jnp
from jax import lax
from jax.sharding import PartitionSpec as P

CX = 16
CY = 16
CZ = 256
MARK_DEV = 1024


lattice_speeds = (
    (0, 0, 0),
    (1, 0, 0),
    (-1, 0, 0),
    (0, 1, 0),
    (0, -1, 0),
    (0, 0, 1),
    (0, 0, -1),
    (1, 1, 0),
    (-1, -1, 0),
    (1, -1, 0),
    (-1, 1, 0),
    (1, 0, 1),
    (-1, 0, -1),
    (1, 0, -1),
    (-1, 0, 1),
    (0, 1, 1),
    (0, -1, -1),
    (0, 1, -1),
    (0, -1, 1),
)
lattice_weights = (1.0 / 3.0,) + (1.0 / 18.0,) * 6 + (1.0 / 36.0,) * 12
relaxation = 0.8
highest = lax.Precision.HIGHEST
three_pass = lax.Precision.HIGH


def extended_2(cells, sides, width):
    for axis, dim in sides:
        count = lax.axis_size(axis)
        head = lax.slice_in_dim(cells, 0, width, axis=dim)
        tail = lax.slice_in_dim(cells, cells.shape[dim] - width, cells.shape[dim], axis=dim)
        cells = jnp.concatenate(
            [
                lax.ppermute(tail, axis, [(i, (i + 1) % count) for i in range(count)]),
                cells,
                lax.ppermute(head, axis, [((i + 1) % count, i) for i in range(count)]),
            ],
            axis=dim,
        )
    return cells


def pass_axis(fields, axis, dim):
    count = lax.axis_size(axis)
    extent = fields[0].shape[dim]
    up = [i for i in range(len(fields)) if lattice_speeds[i][dim] == 1]
    down = [i for i in range(len(fields)) if lattice_speeds[i][dim] == -1]
    going_up = jnp.stack([lax.slice_in_dim(fields[i], extent - 1, extent, axis=dim) for i in up])
    going_down = jnp.stack([lax.slice_in_dim(fields[i], 0, 1, axis=dim) for i in down])
    from_low = lax.ppermute(going_up, axis, [(i, (i + 1) % count) for i in range(count)])
    from_high = lax.ppermute(going_down, axis, [((i + 1) % count, i) for i in range(count)])
    fields = list(fields)
    for k, i in enumerate(up):
        kept = lax.slice_in_dim(fields[i], 0, extent - 1, axis=dim)
        fields[i] = jnp.concatenate([from_low[k], kept], axis=dim)
    for k, i in enumerate(down):
        kept = lax.slice_in_dim(fields[i], 1, extent, axis=dim)
        fields[i] = jnp.concatenate([kept, from_high[k]], axis=dim)
    return fields


def kernel_weights(offset):
    root_term = jnp.sqrt(1.0 + 4.0 * offset - 4.0 * offset * offset)
    return jnp.stack(
        [
            (3.0 - 2.0 * offset - root_term) / 8.0,
            (3.0 - 2.0 * offset + root_term) / 8.0,
            (1.0 + 2.0 * offset + root_term) / 8.0,
            (1.0 + 2.0 * offset - root_term) / 8.0,
        ]
    )


def collide(populations, forcing):
    density = jnp.sum(populations, axis=0)
    velocity = []
    for component in range(3):
        running = 0.5 * forcing[component]
        for direction in range(19):
            speed_value = lattice_speeds[direction][component]
            if speed_value != 0:
                running = running + speed_value * populations[direction]
        velocity.append(running / density)
    square = velocity[0] * velocity[0] + velocity[1] * velocity[1] + velocity[2] * velocity[2]
    collided = []
    for direction in range(19):
        speeds = lattice_speeds[direction]
        weight = lattice_weights[direction]
        contracted = jnp.zeros_like(density)
        for component in range(3):
            if speeds[component] != 0:
                contracted = contracted + speeds[component] * velocity[component]
        equilibrium = (
            weight
            * density
            * (1.0 + 3.0 * contracted + 4.5 * contracted * contracted - 1.5 * square)
        )
        source = jnp.zeros_like(density)
        for component in range(3):
            source = (
                source
                + (
                    3.0 * (speeds[component] - velocity[component])
                    + 9.0 * contracted * speeds[component]
                )
                * forcing[component]
            )
        present = populations[direction]
        collided.append(
            present
            - (present - equilibrium) / relaxation
            + (1.0 - 0.5 / relaxation) * weight * source
        )
    return (collided, jnp.stack(velocity))


def fold_ghost(ghost, sides, extents):
    for (axis, dim), extent in zip(sides, extents):
        count = lax.axis_size(axis)
        below = lax.slice_in_dim(ghost, 0, 1, axis=dim)
        above = lax.slice_in_dim(ghost, extent + 1, extent + 3, axis=dim)
        from_high = lax.ppermute(below, axis, [((i + 1) % count, i) for i in range(count)])
        from_low = lax.ppermute(above, axis, [(i, (i + 1) % count) for i in range(count)])
        low_pad = [(0, 0)] * ghost.ndim
        low_pad[dim] = (0, extent - 2)
        high_pad = [(0, 0)] * ghost.ndim
        high_pad[dim] = (extent - 1, 0)
        ghost = (
            lax.slice_in_dim(ghost, 1, extent + 1, axis=dim)
            + jnp.pad(from_low, low_pad)
            + jnp.pad(from_high, high_pad)
        )
    return ghost


def fold_rims(extended, which, extent):
    middle = lax.slice_in_dim(extended, 3, extent + 3, axis=which)
    low_rims = lax.slice_in_dim(extended, 0, 2, axis=which)
    high_rims = lax.slice_in_dim(extended, extent + 5, extent + 6, axis=which)
    low_pad = [(0, 0)] * extended.ndim
    low_pad[which] = (0, extent - 2)
    high_pad = [(0, 0)] * extended.ndim
    high_pad[which] = (extent - 1, 0)
    return middle + jnp.pad(low_rims, low_pad) + jnp.pad(high_rims, high_pad)


def band_matrix(coordinate, weight, extent, anchor):
    positions = lax.broadcasted_iota(jnp.int32, (coordinate.shape[0], extent), 1)
    running = jnp.zeros((coordinate.shape[0], extent), jnp.float32)
    for shift_step in range(4):
        running = running + jnp.where(
            positions == (coordinate + anchor + shift_step)[:, None],
            weight[shift_step][:, None],
            0.0,
        )
    return running


def spread_banded(forces, coordinates, weights, grid_sizes):
    band_first = band_matrix(coordinates[0], weights[0], grid_sizes[0], 0)
    band_second = band_matrix(coordinates[1], weights[1], grid_sizes[1], 0)
    band_third = band_matrix(coordinates[2], weights[2], grid_sizes[2], 0)
    slots = forces.shape[1]
    plane = (band_first[:, :, None] * band_second[:, None, :]).reshape(slots, -1)
    line = (forces.T[:, :, None] * band_third[:, None, :]).reshape(slots, -1)
    plane, line = lax.optimization_barrier((plane, line))
    product = lax.dot_general(
        plane,
        line,
        (((0,), (0,)), ((), ())),
        precision=three_pass,
        preferred_element_type=jnp.float32,
    )
    product = product.reshape(grid_sizes[0], grid_sizes[1], 3, grid_sizes[2])
    return jnp.transpose(product, (2, 0, 1, 3))


def sample_banded(velocity_ext, coordinates, weights, grid_sizes):
    band_first = band_matrix(coordinates[0], weights[0], grid_sizes[0], 1)
    band_second = band_matrix(coordinates[1], weights[1], grid_sizes[1], 1)
    band_third = band_matrix(coordinates[2], weights[2], grid_sizes[2], 1)
    slots = band_first.shape[0]
    plane = (band_first[:, :, None] * band_second[:, None, :]).reshape(slots, -1)
    plane = lax.optimization_barrier(plane)
    flat_velocity = jnp.transpose(velocity_ext, (1, 2, 0, 3)).reshape(
        grid_sizes[0] * grid_sizes[1], 3 * grid_sizes[2]
    )
    contracted = jnp.dot(
        plane, flat_velocity, precision=three_pass, preferred_element_type=jnp.float32
    )
    contracted = contracted.reshape(slots, 3, grid_sizes[2])
    return jnp.sum(contracted * band_third[:, None, :], axis=2).T


def shards(populations, marker_force, marker_offset, marker_owner, marker_cell):
    count_first = lax.axis_size("gx")
    count_rest = lax.axis_size("gy") * lax.axis_size("gz")
    devices = count_first * count_rest
    capacity = max(4, 2 * MARK_DEV // devices)
    slot_count = devices * capacity
    owners = marker_owner[:, 0]
    row_order = lax.broadcasted_iota(jnp.int32, (MARK_DEV, MARK_DEV), 0)
    column_order = lax.broadcasted_iota(jnp.int32, (MARK_DEV, MARK_DEV), 1)
    earlier = (owners[:, None] == owners[None, :]) & (column_order < row_order)
    before = jnp.sum(earlier.astype(jnp.int32), axis=1)
    slot_index = owners * capacity + before
    placing = (
        slot_index[:, None] == lax.broadcasted_iota(jnp.int32, (MARK_DEV, slot_count), 1)
    ).astype(jnp.float32)
    record = jnp.concatenate(
        [marker_offset, marker_force, marker_cell.astype(jnp.float32)[None, :]], axis=0
    )
    buckets = jnp.dot(record, placing, precision=highest, preferred_element_type=jnp.float32)
    buckets = buckets.reshape(7, count_first, count_rest, capacity)
    received = lax.all_to_all(
        lax.all_to_all(buckets, ("gy", "gz"), split_axis=2, concat_axis=2, tiled=True),
        "gx",
        split_axis=1,
        concat_axis=1,
        tiled=True,
    )
    received = received.reshape(7, slot_count)
    forces = received[3:6]
    cell_index = received[6].astype(jnp.int32)
    coordinates = (cell_index // (CY * CZ), cell_index // CZ % CY, cell_index % CZ)
    weights = (
        kernel_weights(received[0]),
        kernel_weights(received[1]),
        kernel_weights(received[2]),
    )
    ghost_sizes = (CX + 3, CY + 3, CZ + 3)
    halo_sizes = (CX + 4, CY + 4, CZ + 4)
    ghost_field = spread_banded(forces, coordinates, weights, ghost_sizes)
    forcing = fold_ghost(ghost_field, (("gx", 1), ("gy", 2), ("gz", 3)), (CX, CY, CZ))
    collided, velocity = collide(populations, forcing)
    velocity_ext = extended_2(velocity, (("gx", 1), ("gy", 2), ("gz", 3)), 2)
    passed = collided
    for axis, dim in (("gx", 0), ("gy", 1), ("gz", 2)):
        passed = pass_axis(passed, axis, dim)
    new_populations = jnp.stack(passed)
    sampled = sample_banded(velocity_ext, coordinates, weights, halo_sizes)
    sampled = sampled.reshape(3, count_first, count_rest, capacity)
    returned = lax.all_to_all(
        lax.all_to_all(sampled, ("gy", "gz"), split_axis=2, concat_axis=2, tiled=True),
        "gx",
        split_axis=1,
        concat_axis=1,
        tiled=True,
    )
    returned = returned.reshape(3, slot_count)
    marker_velocity = jnp.dot(
        returned, placing.T, precision=highest, preferred_element_type=jnp.float32
    )
    return (new_populations, marker_velocity)


def solution(mesh):
    return jax.shard_map(
        shards,
        mesh=mesh,
        in_specs=(
            P(None, "gx", "gy", "gz"),
            P(None, ("gx", "gy", "gz")),
            P(None, ("gx", "gy", "gz")),
            P(("gx", "gy", "gz"), None),
            P(("gx", "gy", "gz")),
        ),
        out_specs=(P(None, "gx", "gy", "gz"), P(None, ("gx", "gy", "gz"))),
        check_vma=False,
    )
```
